512 devices in a mesh: dp: 16 (over y, core), ctx: 32 (over z, x).
Axes of the slice: x: 4, y: 8, z: 8, core: 2. Of those that a mesh axis runs over, the one named last changes fastest.
Arguments:
- inner_gate: bfloat16 [65536, 1024], P(('dp', 'ctx')), parts along dimension 0, may hold values from -6 to 6
- outer_gate: bfloat16 [65536, 1024], P(('dp', 'ctx')), parts along dimension 0, may hold values from -6 to 6
- signal: bfloat16 [65536, 1024], P(('dp', 'ctx')), parts along dimension 0, may hold values from -6 to 6
- filters: float32 [64, 128], replicated, may hold values from -0.5 to 0.5
- bypass: float32 [1024], replicated, may hold values from 0.5 to 1.5
- query_rows: bfloat16 [65536, 1024], P(('dp', 'ctx')), parts along dimension 0, may hold values from -25 to 25
- key_rows: bfloat16 [65536, 1024], P(('dp', 'ctx')), parts along dimension 0, may hold values from -4.5 to 4.5
Outputs:
- hyena_out: bfloat16 [65536, 1024], P(('dp', 'ctx')), parts along dimension 0
- attended: bfloat16 [65536, 1024], P(('dp', 'ctx')), parts along dimension 0
The draws below stay inside these ranges and needn't reach their ends.
There are 16 independent parts, one for each index of `dp`. The reference program is written for one: setup_inputs(seed, part) draws one part's arguments, and reference() takes and returns one part's arrays. A program takes and returns all parts, laid end to end along the dimension named above; an argument that names none is the same for every part. Nothing has to cross between parts.
All inputs are finite; a program needn't handle non-finite values.
Results may differ from the reference program's by a relative error of at most 0.006.
Values may be sent and summed in bfloat16 or wider, within the bound.
No kernel may reach another device: no remote copies, remote signals or barrier semaphores. Data moves between devices by JAX's collectives and lax.ppermute only.
A program may use at most 128 MiB of HBM per device.

```python
import math
import jax
import jax.numpy as jnp
from jax import lax

HEADS = 8
DH = 128
GROUP = 16
TAPS = 128
CH = 1024
GROUPS = 64
SEQ = 4096


def draw_query_rows(key, part):
    normal = jax.random.normal(jax.random.fold_in(key, 3), (SEQ, HEADS, DH), jnp.float32)
    values = 2.0 * jnp.clip(normal, -3.0, 3.0)
    return values.reshape(SEQ, HEADS * DH).astype(jnp.bfloat16)


def draw_key_rows(key, part):
    normal = jax.random.normal(jax.random.fold_in(key, 5), (SEQ, HEADS, DH), jnp.float32)
    values = jnp.clip(normal, -4.5, 4.5)
    return values.reshape(SEQ, HEADS * DH).astype(jnp.bfloat16)


def level_of(key, shape, split, low, high):
    level, own = 1.0, jax.random.fold_in(key, 6)
    for axis_at, shards_of in split:
        steps = jnp.exp(jax.random.uniform(jax.random.fold_in(own, axis_at), (shards_of,), jnp.float32, low / len(split), high / len(split)))
        level = level * jnp.repeat(steps, shape[axis_at] // shards_of).reshape([-1 if axis == axis_at else 1 for axis in range(len(shape))])
    return level


def noise(stream_key, extent, width, bound, pieces=(), kind=jnp.bfloat16):
    values = width * jax.random.normal(stream_key, extent, jnp.float32)
    if pieces:
        values = values * level_of(stream_key, extent, pieces, -0.22, 0.18)
    return jnp.clip(values, -bound, bound).astype(kind)


def setup_inputs(seed: int = 0, part: int = 0) -> dict:
    key_list = jax.random.split(jax.random.key(seed), 8)
    part_keys = jax.random.split(jax.random.fold_in(key_list[7], part), 8)
    return {
        "inner_gate": noise(part_keys[0], (SEQ, CH), 1.0, 6.0, ((0, 32),)),
        "outer_gate": noise(part_keys[1], (SEQ, CH), 1.0, 6.0, ((0, 32),)),
        "signal": noise(part_keys[2], (SEQ, CH), 1.0, 6.0, ((0, 32),)),
        "filters": noise(key_list[3], (GROUPS, TAPS), 0.09, 0.5, (), jnp.float32),
        "bypass": jnp.clip(jax.random.uniform(key_list[4], (CH,), jnp.float32, 0.5, 1.5), 0.5, 1.5),
        "query_rows": draw_query_rows(jax.random.fold_in(jax.random.fold_in(key_list[7], part), 71), part),
        "key_rows": draw_key_rows(jax.random.fold_in(jax.random.fold_in(key_list[7], part), 71), part),
    }


def reference(inner_gate, outer_gate, signal, filters, bypass, query_rows, key_rows):
    product = lax.optimization_barrier((inner_gate.astype(jnp.float32) * signal.astype(jnp.float32)).astype(jnp.bfloat16))
    product_wide = product.astype(jnp.float32)
    padded = jnp.pad(product_wide, ((TAPS - 1, 0), (0, 0)))
    taps_by_row = jnp.repeat(filters, GROUP, axis=0).T

    def add_tap(tap_index, summed):
        tap_index = jnp.asarray(tap_index).astype(jnp.int32)
        first_row = (TAPS - 1 - tap_index).astype(jnp.int32)
        shifted = lax.dynamic_slice_in_dim(padded, first_row, SEQ, 0)
        column = lax.dynamic_index_in_dim(taps_by_row, tap_index, 0, keepdims=False)
        return summed + shifted * column[None, :]
    convolved = lax.fori_loop(0, TAPS, add_tap, jnp.zeros((SEQ, CH), jnp.float32))
    hyena_out = (outer_gate.astype(jnp.float32) * (convolved + bypass[None, :] * product_wide)).astype(jnp.bfloat16)
    inv_root = 1.0 / math.sqrt(DH)
    block_rows = min(512, SEQ)
    head_queries = query_rows.astype(jnp.float32).reshape(SEQ, HEADS, DH).transpose(1, 0, 2)
    head_keys = key_rows.astype(jnp.float32).reshape(SEQ, HEADS, DH).transpose(1, 0, 2)
    head_values = hyena_out.astype(jnp.float32).reshape(SEQ, HEADS, DH).transpose(1, 0, 2)
    positions = jnp.arange(SEQ, dtype=jnp.int32)

    def one_head(head_items):
        queries_here, keys_here, values_here = head_items

        def one_block(block_index):
            block_index = block_index.astype(jnp.int32)
            query_block = lax.dynamic_slice_in_dim(queries_here, block_index * block_rows, block_rows, 0)
            row_pos = block_index * block_rows + jnp.arange(block_rows, dtype=jnp.int32)
            scores = jnp.dot(query_block, keys_here.T, precision=lax.Precision.HIGHEST) * inv_root
            visible = positions[None, :] <= row_pos[:, None]
            scores = jnp.where(visible, scores, -1e+30)
            highest = lax.optimization_barrier(jnp.max(scores, axis=1, keepdims=True))
            weights = jnp.where(visible, jnp.exp(scores - highest), 0.0)
            weight_sum = lax.optimization_barrier(jnp.sum(weights, axis=1, keepdims=True))
            rounded = lax.optimization_barrier(weights.astype(jnp.bfloat16)).astype(jnp.float32)
            return jnp.dot(rounded, values_here, precision=lax.Precision.HIGHEST) / weight_sum
        return lax.map(one_block, jnp.arange(SEQ // block_rows, dtype=jnp.int32)).reshape(SEQ, DH)
    head_outputs = lax.map(one_head, (head_queries, head_keys, head_values))
    attended = head_outputs.transpose(1, 0, 2).reshape(SEQ, CH).astype(jnp.bfloat16)
    return (hyena_out, attended)
```

```python
import math

import numpy as np
import jax
import jax.numpy as jnp
from jax import lax
from jax.sharding import Mesh, PartitionSpec as P
from jax.experimental import pallas as pl
from jax.experimental.pallas import tpu as pltpu

DH = 128
TAPS = 128


def banded_halves(filters, window_rows):
    group_count, taps = filters.shape
    flipped = filters[:, ::-1]
    padded = jnp.concatenate([flipped, jnp.zeros((group_count, taps), jnp.float32)], axis=1)
    hi = padded.astype(jnp.bfloat16)
    lo = (padded - hi.astype(jnp.float32)).astype(jnp.bfloat16)

    def band(half):
        return jnp.tile(half, (1, taps))[:, : taps * window_rows].reshape(
            group_count, taps, window_rows
        )

    return band(hi), band(lo)


def attend_kernel(x_ref, q_ref, k_ref, v_ref, o_ref, *, nx):
    x = x_ref[0]
    blocks, rows, _ = q_ref.shape
    inv_root = 1.0 / math.sqrt(DH)
    for i in range(blocks):
        length = (i + 1) * nx * rows
        q = q_ref[i]
        k = k_ref[:length, :]
        s = lax.dot_general(
            q, k, (((1,), (1,)), ((), ())), preferred_element_type=jnp.float32
        ) * inv_root
        qpos = (i * nx + x) * rows + lax.broadcasted_iota(jnp.int32, (rows, length), 0)
        kpos = lax.broadcasted_iota(jnp.int32, (rows, length), 1)
        visible = kpos <= qpos
        s = jnp.where(visible, s, -1e30)
        highest = jnp.max(s, axis=1, keepdims=True)
        w = jnp.where(visible, jnp.exp(s - highest), 0.0)
        total = jnp.sum(w, axis=1, keepdims=True)
        o = jnp.dot(w.astype(jnp.bfloat16), v_ref[:length, :], preferred_element_type=jnp.float32)
        o_ref[i] = (o / total).astype(o_ref.dtype)


def attend_local(x_index, q, k, v, nx):
    blocks, rows, dh = q.shape
    seq = k.shape[0]
    flops = 2 * 2 * blocks * rows * seq * dh // 2
    return pl.pallas_call(
        lambda *refs: attend_kernel(*refs, nx=nx),
        out_shape=jax.ShapeDtypeStruct(q.shape, jnp.bfloat16),
        in_specs=[
            pl.BlockSpec(memory_space=pltpu.SMEM),
            pl.BlockSpec(memory_space=pltpu.VMEM),
            pl.BlockSpec(memory_space=pltpu.VMEM),
            pl.BlockSpec(memory_space=pltpu.VMEM),
        ],
        out_specs=pl.BlockSpec(memory_space=pltpu.VMEM),
        compiler_params=pltpu.CompilerParams(vmem_limit_bytes=48 * 1024 * 1024),
        cost_estimate=pl.CostEstimate(
            flops=flops,
            transcendentals=blocks * rows * seq // 2,
            bytes_accessed=2 * (q.size * 2 + k.size + v.size),
        ),
    )(x_index, q, k, v)


def shards(inner_gate, outer_gate, signal, filters, bypass, query_rows, key_rows):
    local_rows, channels = signal.shape
    nz = lax.axis_size("cz")
    nx = lax.axis_size("cx")
    members = nz * nx
    heads = channels // DH
    my_x = lax.axis_index("cx")

    product = (inner_gate.astype(jnp.float32) * signal.astype(jnp.float32)).astype(jnp.bfloat16)
    left_rim = lax.ppermute(
        product[local_rows - (TAPS - 1) :],
        ("cz", "cx"),
        [(i, i + 1) for i in range(members - 1)],
    )
    extended = jnp.concatenate([left_rim, product], axis=0)
    group_count = filters.shape[0]
    group_width = channels // group_count
    window_rows = local_rows + TAPS - 1
    band_hi, band_lo = banded_halves(filters, window_rows)
    windows = extended.reshape(window_rows, group_count, group_width)
    convolved = jnp.einsum(
        "gtj,jgc->tgc", band_hi, windows, preferred_element_type=jnp.float32
    ) + jnp.einsum("gtj,jgc->tgc", band_lo, windows, preferred_element_type=jnp.float32)
    convolved = convolved.reshape(local_rows, channels)
    hyena_out = (
        outer_gate.astype(jnp.float32) * (convolved + bypass[None, :] * product.astype(jnp.float32))
    ).astype(jnp.bfloat16)

    def by_head(a):
        return a.reshape(local_rows, heads, DH).transpose(1, 0, 2)

    stacked = jnp.stack([by_head(query_rows), by_head(key_rows), by_head(hyena_out)])
    spread = lax.all_to_all(stacked, "cz", 1, 1, tiled=True)
    q_here = spread[0]
    kv = lax.all_gather(spread[1:], "cx", axis=2, tiled=False)
    kv = kv.reshape(2, members * local_rows, DH)
    x_index = jnp.reshape(my_x, (1,)).astype(jnp.int32)
    out_here = attend_local(x_index, q_here, kv[0], kv[1], nx)
    returned = lax.all_to_all(out_here, "cz", 0, 0, tiled=True)
    attended = returned.transpose(1, 0, 2).reshape(local_rows, channels)
    return (hyena_out, attended)


def ctx_split(mesh):
    devices = np.asarray(mesh.devices)
    row = devices[0]
    try:
        nx = len({d.coords[0] for d in row})
    except Exception:
        nx = 4
    if row.size % nx:
        nx = 1
    return Mesh(devices.reshape(devices.shape[0], row.size // nx, nx), ("dp", "cz", "cx"))


def solution(mesh):
    split = ctx_split(mesh)
    rows = P(("dp", "cz", "cx"), None)
    placed = (rows, rows, rows, P(), P(), rows, rows)
    return jax.shard_map(
        shards,
        mesh=split,
        in_specs=placed,
        out_specs=(rows, rows),
        check_vma=False,
    )
```

```python
import math

import numpy as np
import jax
import jax.numpy as jnp
from jax import lax
from jax.sharding import Mesh, PartitionSpec as P
from jax.experimental import pallas as pl
from jax.experimental.pallas import tpu as pltpu

DH = 128
TAPS = 128


def shifted(array, axis, by):
    n = lax.axis_size(axis)
    return lax.ppermute(array, axis, [(i, (i + by) % n) for i in range(n)])


def exchange(blocks, axis):
    n = lax.axis_size(axis)
    me = lax.axis_index(axis)
    doubled = jnp.concatenate([blocks, blocks], axis=0)
    rot = lax.dynamic_slice_in_dim(doubled, me, n, 0)
    recv = [rot[0]] + [shifted(rot[k], axis, k) for k in range(1, n)]
    back = jnp.stack(recv[::-1])
    doubled_back = jnp.concatenate([back, back], axis=0)
    return lax.dynamic_slice_in_dim(doubled_back, n - 1 - me, n, 0)


def banded_halves(filters, window_rows, out_rows):
    group_count, taps = filters.shape
    flipped = filters[:, ::-1]
    hi = flipped.astype(jnp.bfloat16)
    lo = (flipped - hi.astype(jnp.float32)).astype(jnp.bfloat16)
    d = lax.broadcasted_iota(jnp.int32, (taps, out_rows, window_rows), 0)
    t = lax.broadcasted_iota(jnp.int32, (taps, out_rows, window_rows), 1)
    j = lax.broadcasted_iota(jnp.int32, (taps, out_rows, window_rows), 2)
    one_hot = (j - t == d).astype(jnp.bfloat16)

    def band(half):
        return jnp.einsum(
            "gd,dtj->gtj", half, one_hot, preferred_element_type=jnp.float32
        ).astype(jnp.bfloat16)

    return band(hi), band(lo)


def attend_kernel(x_ref, q_ref, *refs, nx):
    k_refs = refs[:nx]
    v_refs = refs[nx : 2 * nx]
    o_ref = refs[2 * nx]
    x = x_ref[0]
    blocks, rows, dh = q_ref.shape
    inv_root = 1.0 / math.sqrt(DH)
    for i in range(blocks):
        length = (i + 1) * rows
        q = q_ref[i]
        qpos = (i * nx + x) * rows + lax.broadcasted_iota(jnp.int32, (rows, length), 0)
        col = lax.broadcasted_iota(jnp.int32, (rows, length), 1)
        pieces = []
        for d in range(nx):
            xd = lax.rem(x + d, nx)
            k = k_refs[d][: i + 1].reshape(length, dh)
            s = lax.dot_general(
                q, k, (((1,), (1,)), ((), ())), preferred_element_type=jnp.float32
            ) * inv_root
            kpos = ((col // rows) * nx + xd) * rows + lax.rem(col, rows)
            visible = kpos <= qpos
            pieces.append((jnp.where(visible, s, -1e30), visible))
        highest = jnp.max(pieces[0][0], axis=1, keepdims=True)
        for s, _ in pieces[1:]:
            highest = jnp.maximum(highest, jnp.max(s, axis=1, keepdims=True))
        total = None
        acc = None
        for d, (s, visible) in enumerate(pieces):
            w = jnp.where(visible, jnp.exp(s - highest), 0.0)
            part_sum = jnp.sum(w, axis=1, keepdims=True)
            v = v_refs[d][: i + 1].reshape(length, dh)
            part = jnp.dot(w.astype(jnp.bfloat16), v, preferred_element_type=jnp.float32)
            total = part_sum if total is None else total + part_sum
            acc = part if acc is None else acc + part
        o_ref[i] = (acc / total).astype(o_ref.dtype)


def attend_local(x_index, q, ks, vs, nx):
    blocks, rows, dh = q.shape
    seq = nx * blocks * rows
    flops = 2 * 2 * blocks * rows * seq * dh // 2
    vmem = pl.BlockSpec(memory_space=pltpu.VMEM)
    return pl.pallas_call(
        lambda *refs: attend_kernel(*refs, nx=nx),
        out_shape=jax.ShapeDtypeStruct(q.shape, jnp.bfloat16),
        in_specs=[pl.BlockSpec(memory_space=pltpu.SMEM)] + [vmem] * (1 + 2 * nx),
        out_specs=vmem,
        compiler_params=pltpu.CompilerParams(vmem_limit_bytes=48 * 1024 * 1024),
        cost_estimate=pl.CostEstimate(
            flops=flops,
            transcendentals=blocks * rows * seq // 2,
            bytes_accessed=2 * (2 * q.size + 2 * seq * dh),
        ),
    )(x_index, q, *ks, *vs)


def gather_x(kv, nx):
    if nx == 4:
        from_left = shifted(kv, "cx", 1)
        from_right = shifted(kv, "cx", -1)
        relay_k = shifted(from_right[0], "cx", -1)
        relay_v = shifted(from_left[1], "cx", 1)
        ks = [kv[0], from_right[0], relay_k, from_left[0]]
        vs = [kv[1], from_right[1], relay_v, from_left[1]]
        return ks, vs
    got = [kv] + [shifted(kv, "cx", -d) for d in range(1, nx)]
    return [g[0] for g in got], [g[1] for g in got]


def shards(inner_gate, outer_gate, signal, filters, bypass, query_rows, key_rows):
    local_rows, channels = signal.shape
    nz = lax.axis_size("cz")
    nx = lax.axis_size("cx")
    members = nz * nx
    heads = channels // DH
    my_x = lax.axis_index("cx")

    product = (inner_gate.astype(jnp.float32) * signal.astype(jnp.float32)).astype(jnp.bfloat16)
    left_rim = lax.ppermute(
        product[local_rows - (TAPS - 1) :],
        ("cz", "cx"),
        [(i, i + 1) for i in range(members - 1)],
    )
    window_rows = local_rows + TAPS
    extended = jnp.concatenate(
        [left_rim, product, jnp.zeros((1, channels), jnp.bfloat16)], axis=0
    )
    group_count = filters.shape[0]
    group_width = channels // group_count
    band_hi, band_lo = banded_halves(filters, window_rows, local_rows)
    windows = extended.reshape(window_rows, group_count, group_width)
    convolved = jnp.einsum(
        "gtj,jgc->tgc", band_hi, windows, preferred_element_type=jnp.float32
    ) + jnp.einsum("gtj,jgc->tgc", band_lo, windows, preferred_element_type=jnp.float32)
    convolved = convolved.reshape(local_rows, channels)
    hyena_out = (
        outer_gate.astype(jnp.float32) * (convolved + bypass[None, :] * product.astype(jnp.float32))
    ).astype(jnp.bfloat16)

    def by_head(a):
        return a.reshape(local_rows, heads, DH).transpose(1, 0, 2)

    stacked = jnp.stack([by_head(query_rows), by_head(key_rows), by_head(hyena_out)], axis=1)
    spread = exchange(stacked, "cz")
    q_here = spread[:, 0]
    kv = jnp.stack([spread[:, 1], spread[:, 2]])
    ks, vs = gather_x(kv, nx)
    x_index = jnp.reshape(my_x, (1,)).astype(jnp.int32)
    out_here = attend_local(x_index, q_here, ks, vs, nx)
    returned = exchange(out_here, "cz")
    attended = returned.transpose(1, 0, 2).reshape(local_rows, channels)
    return (hyena_out, attended)


def ctx_split(mesh):
    devices = np.asarray(mesh.devices)
    row = devices[0]
    try:
        nx = len({d.coords[0] for d in row})
    except Exception:
        nx = 4
    if row.size % nx:
        nx = 1
    return Mesh(devices.reshape(devices.shape[0], row.size // nx, nx), ("dp", "cz", "cx"))


def solution(mesh):
    split = ctx_split(mesh)
    rows = P(("dp", "cz", "cx"), None)
    placed = (rows, rows, rows, P(), P(), rows, rows)
    return jax.shard_map(
        shards,
        mesh=split,
        in_specs=placed,
        out_specs=(rows, rows),
        check_vma=False,
    )
```

```python
import math

import numpy as np
import jax
import jax.numpy as jnp
from jax import lax
from jax.sharding import Mesh, PartitionSpec as P
from jax.experimental import pallas as pl
from jax.experimental.pallas import tpu as pltpu

DH = 128
TAPS = 128


def shifted(array, axis, by):
    n = lax.axis_size(axis)
    return lax.ppermute(array, axis, [(i, (i + by) % n) for i in range(n)])


def exchange(blocks, axis):
    n = lax.axis_size(axis)
    me = lax.axis_index(axis)
    doubled = jnp.concatenate([blocks, blocks], axis=0)
    rot = lax.dynamic_slice_in_dim(doubled, me, n, 0)
    recv = [rot[0]] + [shifted(rot[k], axis, k) for k in range(1, n)]
    back = jnp.stack(recv[::-1])
    doubled_back = jnp.concatenate([back, back], axis=0)
    return lax.dynamic_slice_in_dim(doubled_back, n - 1 - me, n, 0)


def conv_kernel(ext_ref, pads_ref, outer_ref, bypass_ref, out_ref, *, taps, group_width):
    window, channels = ext_ref.shape
    rows = out_ref.shape[0]
    groups_per_chunk = 128 // group_width
    lane_group = lax.broadcasted_iota(jnp.int32, (rows, 128), 1) // group_width

    def chunk(k, carry):
        col = pl.multiple_of(k * 128, 128)
        x = ext_ref[:, pl.ds(col, 128)]
        acc = jnp.zeros((rows, 128), jnp.float32)
        for gg in range(groups_per_chunk):
            g = k * groups_per_chunk + gg
            row = pads_ref[pl.ds(g, 1), :]
            band = pltpu.roll(jnp.broadcast_to(row, (rows, window)), 0, 1, stride=1, stride_axis=0)
            hi = band.astype(jnp.bfloat16)
            lo = (band - hi.astype(jnp.float32)).astype(jnp.bfloat16)
            y = jnp.dot(hi, x, preferred_element_type=jnp.float32) + jnp.dot(
                lo, x, preferred_element_type=jnp.float32
            )
            acc = jnp.where(lane_group == gg, y, acc)
        product = ext_ref[pl.ds(taps - 1, rows), pl.ds(col, 128)].astype(jnp.float32)
        outer = outer_ref[:, pl.ds(col, 128)].astype(jnp.float32)
        bypass = bypass_ref[:, pl.ds(col, 128)]
        out_ref[:, pl.ds(col, 128)] = (outer * (acc + bypass * product)).astype(out_ref.dtype)
        return carry

    lax.fori_loop(0, channels // 128, chunk, 0)


def hyena_local(ext, filters, outer, bypass, taps):
    rows, channels = outer.shape
    window = ext.shape[0]
    group_count = filters.shape[0]
    pads = jnp.concatenate(
        [filters[:, ::-1], jnp.zeros((group_count, window - taps), jnp.float32)], axis=1
    )
    vmem = pl.BlockSpec(memory_space=pltpu.VMEM)
    return pl.pallas_call(
        lambda *refs: conv_kernel(*refs, taps=taps, group_width=channels // group_count),
        out_shape=jax.ShapeDtypeStruct((rows, channels), jnp.bfloat16),
        in_specs=[vmem] * 4,
        out_specs=vmem,
        cost_estimate=pl.CostEstimate(
            flops=2 * 2 * 8 * rows * window * channels,
            transcendentals=0,
            bytes_accessed=2 * ext.size + 4 * pads.size + 4 * outer.size,
        ),
    )(ext, pads, outer, bypass.reshape(1, channels))


def attend_kernel(x_ref, q_ref, *refs, nx):
    k_refs = refs[:nx]
    v_refs = refs[nx : 2 * nx]
    o_ref = refs[2 * nx]
    x = x_ref[0]
    blocks, rows, dh = q_ref.shape
    inv_root = 1.0 / math.sqrt(DH)
    for i in range(blocks):
        length = (i + 1) * rows
        q = q_ref[i]
        qpos = (i * nx + x) * rows + lax.broadcasted_iota(jnp.int32, (rows, length), 0)
        col = lax.broadcasted_iota(jnp.int32, (rows, length), 1)
        pieces = []
        for d in range(nx):
            xd = lax.rem(x + d, nx)
            k = k_refs[d][: i + 1].reshape(length, dh)
            s = lax.dot_general(
                q, k, (((1,), (1,)), ((), ())), preferred_element_type=jnp.float32
            ) * inv_root
            kpos = ((col // rows) * nx + xd) * rows + lax.rem(col, rows)
            visible = kpos <= qpos
            pieces.append((jnp.where(visible, s, -1e30), visible))
        highest = jnp.max(pieces[0][0], axis=1, keepdims=True)
        for s, _ in pieces[1:]:
            highest = jnp.maximum(highest, jnp.max(s, axis=1, keepdims=True))
        total = None
        acc = None
        for d, (s, visible) in enumerate(pieces):
            w = jnp.where(visible, jnp.exp(s - highest), 0.0)
            part_sum = jnp.sum(w, axis=1, keepdims=True)
            v = v_refs[d][: i + 1].reshape(length, dh)
            part = jnp.dot(w.astype(jnp.bfloat16), v, preferred_element_type=jnp.float32)
            total = part_sum if total is None else total + part_sum
            acc = part if acc is None else acc + part
        o_ref[i] = (acc / total).astype(o_ref.dtype)


def attend_local(x_index, q, ks, vs, nx):
    blocks, rows, dh = q.shape
    seq = nx * blocks * rows
    flops = 2 * 2 * blocks * rows * seq * dh // 2
    vmem = pl.BlockSpec(memory_space=pltpu.VMEM)
    return pl.pallas_call(
        lambda *refs: attend_kernel(*refs, nx=nx),
        out_shape=jax.ShapeDtypeStruct(q.shape, jnp.bfloat16),
        in_specs=[pl.BlockSpec(memory_space=pltpu.SMEM)] + [vmem] * (1 + 2 * nx),
        out_specs=vmem,
        compiler_params=pltpu.CompilerParams(vmem_limit_bytes=48 * 1024 * 1024),
        cost_estimate=pl.CostEstimate(
            flops=flops,
            transcendentals=blocks * rows * seq // 2,
            bytes_accessed=2 * (2 * q.size + 2 * seq * dh),
        ),
    )(x_index, q, *ks, *vs)


def gather_x(kv, nx):
    if nx == 4:
        from_left = shifted(kv, "cx", 1)
        from_right = shifted(kv, "cx", -1)
        relay_k = shifted(from_right[0], "cx", -1)
        relay_v = shifted(from_left[1], "cx", 1)
        ks = [kv[0], from_right[0], relay_k, from_left[0]]
        vs = [kv[1], from_right[1], relay_v, from_left[1]]
        return ks, vs
    got = [kv] + [shifted(kv, "cx", -d) for d in range(1, nx)]
    return [g[0] for g in got], [g[1] for g in got]


def shards(inner_gate, outer_gate, signal, filters, bypass, query_rows, key_rows):
    local_rows, channels = signal.shape
    nz = lax.axis_size("cz")
    nx = lax.axis_size("cx")
    members = nz * nx
    heads = channels // DH
    my_x = lax.axis_index("cx")

    product = (inner_gate.astype(jnp.float32) * signal.astype(jnp.float32)).astype(jnp.bfloat16)
    left_rim = lax.ppermute(
        product[local_rows - (TAPS - 1) :],
        ("cz", "cx"),
        [(i, i + 1) for i in range(members - 1)],
    )
    extended = jnp.concatenate(
        [left_rim, product, jnp.zeros((1, channels), jnp.bfloat16)], axis=0
    )
    hyena_out = hyena_local(extended, filters, outer_gate, bypass, TAPS)

    def by_head(a):
        return a.reshape(local_rows, heads, DH).transpose(1, 0, 2)

    qk = jnp.stack([by_head(query_rows), by_head(key_rows)], axis=1)
    qk_spread = lax.all_to_all(qk, "cz", 0, 0, tiled=True)
    v_spread = lax.all_to_all(by_head(hyena_out), "cz", 0, 0, tiled=True)
    q_here = qk_spread[:, 0]
    kv = jnp.stack([qk_spread[:, 1], v_spread])
    ks, vs = gather_x(kv, nx)
    x_index = jnp.reshape(my_x, (1,)).astype(jnp.int32)
    out_here = attend_local(x_index, q_here, ks, vs, nx)
    returned = lax.all_to_all(out_here, "cz", 0, 0, tiled=True)
    attended = returned.transpose(1, 0, 2).reshape(local_rows, channels)
    return (hyena_out, attended)


def ctx_split(mesh):
    devices = np.asarray(mesh.devices)
    row = devices[0]
    try:
        nx = len({d.coords[0] for d in row})
    except Exception:
        nx = 4
    if row.size % nx:
        nx = 1
    return Mesh(devices.reshape(devices.shape[0], row.size // nx, nx), ("dp", "cz", "cx"))


def solution(mesh):
    split = ctx_split(mesh)
    rows = P(("dp", "cz", "cx"), None)
    placed = (rows, rows, rows, P(), P(), rows, rows)
    return jax.shard_map(
        shards,
        mesh=split,
        in_specs=placed,
        out_specs=(rows, rows),
        check_vma=False,
    )
```

```python
import math

import numpy as np
import jax
import jax.numpy as jnp
from jax import lax
from jax.sharding import Mesh, PartitionSpec as P
from jax.experimental import pallas as pl
from jax.experimental.pallas import tpu as pltpu

DH = 128
TAPS = 128


def shifted(array, axis, by):
    n = lax.axis_size(axis)
    return lax.ppermute(array, axis, [(i, (i + by) % n) for i in range(n)])


def conv_kernel(ext_ref, pads_ref, outer_ref, bypass_ref, out_ref, heads_ref, *, taps, group_width):
    window, channels = ext_ref.shape
    rows = out_ref.shape[0]
    groups_per_chunk = 128 // group_width
    lane_group = lax.broadcasted_iota(jnp.int32, (rows, 128), 1) // group_width

    def chunk(k, carry):
        col = pl.multiple_of(k * 128, 128)
        x = ext_ref[:, pl.ds(col, 128)]
        acc = jnp.zeros((rows, 128), jnp.float32)
        for gg in range(groups_per_chunk):
            g = k * groups_per_chunk + gg
            row = pads_ref[pl.ds(g, 1), :]
            band = pltpu.roll(jnp.broadcast_to(row, (rows, window)), 0, 1, stride=1, stride_axis=0)
            hi = band.astype(jnp.bfloat16)
            lo = (band - hi.astype(jnp.float32)).astype(jnp.bfloat16)
            y = jnp.dot(hi, x, preferred_element_type=jnp.float32) + jnp.dot(
                lo, x, preferred_element_type=jnp.float32
            )
            acc = jnp.where(lane_group == gg, y, acc)
        product = ext_ref[pl.ds(taps - 1, rows), pl.ds(col, 128)].astype(jnp.float32)
        outer = outer_ref[:, pl.ds(col, 128)].astype(jnp.float32)
        bypass = bypass_ref[:, pl.ds(col, 128)]
        result = (outer * (acc + bypass * product)).astype(out_ref.dtype)
        out_ref[:, pl.ds(col, 128)] = result
        heads_ref[k] = result
        return carry

    lax.fori_loop(0, channels // 128, chunk, 0)


def hyena_local(ext, filters, outer, bypass, taps):
    rows, channels = outer.shape
    window = ext.shape[0]
    group_count = filters.shape[0]
    pads = jnp.concatenate(
        [filters[:, ::-1], jnp.zeros((group_count, window - taps), jnp.float32)], axis=1
    )
    vmem = pl.BlockSpec(memory_space=pltpu.VMEM)
    return pl.pallas_call(
        lambda *refs: conv_kernel(*refs, taps=taps, group_width=channels // group_count),
        out_shape=(
            jax.ShapeDtypeStruct((rows, channels), jnp.bfloat16),
            jax.ShapeDtypeStruct((channels // DH, rows, DH), jnp.bfloat16),
        ),
        in_specs=[vmem] * 4,
        out_specs=(vmem, vmem),
        cost_estimate=pl.CostEstimate(
            flops=2 * 2 * 8 * rows * window * channels,
            transcendentals=0,
            bytes_accessed=2 * ext.size + 4 * pads.size + 4 * outer.size,
        ),
    )(ext, pads, outer, bypass.reshape(1, channels))


def attend_kernel(x_ref, q_ref, *refs, nx):
    k_refs = refs[:nx]
    v_refs = refs[nx : 2 * nx]
    o_ref = refs[2 * nx]
    x = x_ref[0]
    blocks, rows, dh = q_ref.shape
    inv_root = 1.0 / math.sqrt(DH)
    for i in range(blocks):
        length = (i + 1) * rows
        q = q_ref[i]
        qpos = (i * nx + x) * rows + lax.broadcasted_iota(jnp.int32, (rows, length), 0)
        col = lax.broadcasted_iota(jnp.int32, (rows, length), 1)
        pieces = []
        for d in range(nx):
            xd = lax.rem(x + d, nx)
            k = k_refs[d][: i + 1].reshape(length, dh)
            s = lax.dot_general(
                q, k, (((1,), (1,)), ((), ())), preferred_element_type=jnp.float32
            ) * inv_root
            kpos = ((col // rows) * nx + xd) * rows + lax.rem(col, rows)
            visible = kpos <= qpos
            pieces.append((jnp.where(visible, s, -1e30), visible))
        highest = jnp.max(pieces[0][0], axis=1, keepdims=True)
        for s, _ in pieces[1:]:
            highest = jnp.maximum(highest, jnp.max(s, axis=1, keepdims=True))
        total = None
        acc = None
        for d, (s, visible) in enumerate(pieces):
            w = jnp.where(visible, jnp.exp(s - highest), 0.0)
            part_sum = jnp.sum(w, axis=1, keepdims=True)
            v = v_refs[d][: i + 1].reshape(length, dh)
            part = jnp.dot(w.astype(jnp.bfloat16), v, preferred_element_type=jnp.float32)
            total = part_sum if total is None else total + part_sum
            acc = part if acc is None else acc + part
        o_ref[i] = (acc / total).astype(o_ref.dtype)


def attend_local(x_index, q, ks, vs, nx):
    blocks, rows, dh = q.shape
    seq = nx * blocks * rows
    flops = 2 * 2 * blocks * rows * seq * dh // 2
    vmem = pl.BlockSpec(memory_space=pltpu.VMEM)
    return pl.pallas_call(
        lambda *refs: attend_kernel(*refs, nx=nx),
        out_shape=jax.ShapeDtypeStruct(q.shape, jnp.bfloat16),
        in_specs=[pl.BlockSpec(memory_space=pltpu.SMEM)] + [vmem] * (1 + 2 * nx),
        out_specs=vmem,
        compiler_params=pltpu.CompilerParams(vmem_limit_bytes=48 * 1024 * 1024),
        cost_estimate=pl.CostEstimate(
            flops=flops,
            transcendentals=blocks * rows * seq // 2,
            bytes_accessed=2 * (2 * q.size + 2 * seq * dh),
        ),
    )(x_index, q, *ks, *vs)


def gather_x(piece, nx):
    if nx == 4:
        half = piece.shape[0] // 2
        from_left = shifted(piece, "cx", 1)
        from_right = shifted(piece, "cx", -1)
        relay_a = shifted(from_right[:half], "cx", -1)
        relay_b = shifted(from_left[half:], "cx", 1)
        return [piece, from_right, jnp.concatenate([relay_a, relay_b], axis=0), from_left]
    return [piece] + [shifted(piece, "cx", -d) for d in range(1, nx)]


def shards(inner_gate, outer_gate, signal, filters, bypass, query_rows, key_rows):
    local_rows, channels = signal.shape
    nz = lax.axis_size("cz")
    nx = lax.axis_size("cx")
    members = nz * nx
    heads = channels // DH
    my_x = lax.axis_index("cx")

    product = (inner_gate.astype(jnp.float32) * signal.astype(jnp.float32)).astype(jnp.bfloat16)
    left_rim = lax.ppermute(
        product[local_rows - (TAPS - 1) :],
        ("cz", "cx"),
        [(i, i + 1) for i in range(members - 1)],
    )
    extended = jnp.concatenate(
        [left_rim, product, jnp.zeros((1, channels), jnp.bfloat16)], axis=0
    )
    hyena_out, v_heads = hyena_local(extended, filters, outer_gate, bypass, TAPS)

    def by_head(a):
        return a.reshape(local_rows, heads, DH).transpose(1, 0, 2)

    qk = jnp.stack([by_head(query_rows), by_head(key_rows)], axis=1)
    qk_spread = lax.all_to_all(qk, "cz", 0, 0, tiled=True)
    q_here = qk_spread[:, 0]
    ks = gather_x(qk_spread[:, 1], nx)
    v_spread = lax.all_to_all(v_heads, "cz", 0, 0, tiled=True)
    vs = gather_x(v_spread, nx)
    x_index = jnp.reshape(my_x, (1,)).astype(jnp.int32)
    out_here = attend_local(x_index, q_here, ks, vs, nx)
    returned = lax.all_to_all(out_here, "cz", 0, 0, tiled=True)
    attended = returned.transpose(1, 0, 2).reshape(local_rows, channels)
    return (hyena_out, attended)


def ctx_split(mesh):
    devices = np.asarray(mesh.devices)
    row = devices[0]
    try:
        nx = len({d.coords[0] for d in row})
    except Exception:
        nx = 4
    if row.size % nx:
        nx = 1
    return Mesh(devices.reshape(devices.shape[0], row.size // nx, nx), ("dp", "cz", "cx"))


def solution(mesh):
    split = ctx_split(mesh)
    rows = P(("dp", "cz", "cx"), None)
    placed = (rows, rows, rows, P(), P(), rows, rows)
    return jax.shard_map(
        shards,
        mesh=split,
        in_specs=placed,
        out_specs=(rows, rows),
        check_vma=False,
    )
```

```python
import math

import numpy as np
import jax
import jax.numpy as jnp
from jax import lax
from jax.sharding import Mesh, PartitionSpec as P
from jax.experimental import pallas as pl
from jax.experimental.pallas import tpu as pltpu

DH = 128
TAPS = 128


def shifted(array, axis, by):
    n = lax.axis_size(axis)
    return lax.ppermute(array, axis, [(i, (i + by) % n) for i in range(n)])


def conv_kernel(ext_ref, pads_ref, outer_ref, bypass_ref, out_ref, heads_ref, *, taps, group_width):
    window, channels = ext_ref.shape
    rows = out_ref.shape[0]
    groups_per_chunk = 128 // group_width
    lane_group = lax.broadcasted_iota(jnp.int32, (rows, 128), 1) // group_width

    def chunk(k, carry):
        col = pl.multiple_of(k * 128, 128)
        x = ext_ref[:, pl.ds(col, 128)]
        acc = jnp.zeros((rows, 128), jnp.float32)
        for gg in range(groups_per_chunk):
            g = k * groups_per_chunk + gg
            row = pads_ref[pl.ds(g, 1), :]
            band = pltpu.roll(jnp.broadcast_to(row, (rows, window)), 0, 1, stride=1, stride_axis=0)
            hi = band.astype(jnp.bfloat16)
            lo = (band - hi.astype(jnp.float32)).astype(jnp.bfloat16)
            y = jnp.dot(hi, x, preferred_element_type=jnp.float32) + jnp.dot(
                lo, x, preferred_element_type=jnp.float32
            )
            acc = jnp.where(lane_group == gg, y, acc)
        product = ext_ref[pl.ds(taps - 1, rows), pl.ds(col, 128)].astype(jnp.float32)
        outer = outer_ref[:, pl.ds(col, 128)].astype(jnp.float32)
        bypass = bypass_ref[:, pl.ds(col, 128)]
        result = (outer * (acc + bypass * product)).astype(out_ref.dtype)
        out_ref[:, pl.ds(col, 128)] = result
        heads_ref[k] = result
        return carry

    lax.fori_loop(0, channels // 128, chunk, 0)


def hyena_local(ext, filters, outer, bypass, taps):
    rows, channels = outer.shape
    window = ext.shape[0]
    group_count = filters.shape[0]
    pads = jnp.concatenate(
        [filters[:, ::-1], jnp.zeros((group_count, window - taps), jnp.float32)], axis=1
    )
    vmem = pl.BlockSpec(memory_space=pltpu.VMEM)
    return pl.pallas_call(
        lambda *refs: conv_kernel(*refs, taps=taps, group_width=channels // group_count),
        out_shape=(
            jax.ShapeDtypeStruct((rows, channels), jnp.bfloat16),
            jax.ShapeDtypeStruct((channels // DH, rows, DH), jnp.bfloat16),
        ),
        in_specs=[vmem] * 4,
        out_specs=(vmem, vmem),
        cost_estimate=pl.CostEstimate(
            flops=2 * 2 * 8 * rows * window * channels,
            transcendentals=0,
            bytes_accessed=2 * ext.size + 4 * pads.size + 4 * outer.size,
        ),
    )(ext, pads, outer, bypass.reshape(1, channels))


def attend_kernel(x_ref, q_ref, *refs, nx):
    k_refs = refs[:nx]
    v_refs = refs[nx : 2 * nx]
    o_ref = refs[2 * nx]
    x = x_ref[0]
    blocks, rows, dh = q_ref.shape
    inv_root = 1.0 / math.sqrt(DH)
    for i in range(blocks):
        length = (i + 1) * rows
        q = q_ref[i]
        qpos = (i * nx + x) * rows + lax.broadcasted_iota(jnp.int32, (rows, length), 0)
        col = lax.broadcasted_iota(jnp.int32, (rows, length), 1)
        pieces = []
        for d in range(nx):
            xd = lax.rem(x + d, nx)
            k = k_refs[d][: i + 1].reshape(length, dh)
            s = lax.dot_general(
                q, k, (((1,), (1,)), ((), ())), preferred_element_type=jnp.float32
            ) * inv_root
            kpos = ((col // rows) * nx + xd) * rows + lax.rem(col, rows)
            visible = kpos <= qpos
            pieces.append((jnp.where(visible, s, -1e30), visible))
        highest = jnp.max(pieces[0][0], axis=1, keepdims=True)
        for s, _ in pieces[1:]:
            highest = jnp.maximum(highest, jnp.max(s, axis=1, keepdims=True))
        total = None
        acc = None
        for d, (s, visible) in enumerate(pieces):
            w = jnp.where(visible, jnp.exp(s - highest), 0.0)
            part_sum = jnp.sum(w, axis=1, keepdims=True)
            v = v_refs[d][: i + 1].reshape(length, dh)
            part = jnp.dot(w.astype(jnp.bfloat16), v, preferred_element_type=jnp.float32)
            total = part_sum if total is None else total + part_sum
            acc = part if acc is None else acc + part
        o_ref[i] = (acc / total).astype(o_ref.dtype)


def attend_local(x_index, q, ks, vs, nx):
    blocks, rows, dh = q.shape
    seq = nx * blocks * rows
    flops = 2 * 2 * blocks * rows * seq * dh // 2
    vmem = pl.BlockSpec(memory_space=pltpu.VMEM)
    return pl.pallas_call(
        lambda *refs: attend_kernel(*refs, nx=nx),
        out_shape=jax.ShapeDtypeStruct(q.shape, jnp.bfloat16),
        in_specs=[pl.BlockSpec(memory_space=pltpu.SMEM)] + [vmem] * (1 + 2 * nx),
        out_specs=vmem,
        compiler_params=pltpu.CompilerParams(vmem_limit_bytes=48 * 1024 * 1024),
        cost_estimate=pl.CostEstimate(
            flops=flops,
            transcendentals=blocks * rows * seq // 2,
            bytes_accessed=2 * (2 * q.size + 2 * seq * dh),
        ),
    )(x_index, q, *ks, *vs)


def gather_x(piece, nx, split_axis=0):
    if nx == 4:
        half = piece.shape[split_axis] // 2
        from_left = shifted(piece, "cx", 1)
        from_right = shifted(piece, "cx", -1)
        relay_a = shifted(lax.slice_in_dim(from_right, 0, half, axis=split_axis), "cx", -1)
        relay_b = shifted(
            lax.slice_in_dim(from_left, half, piece.shape[split_axis], axis=split_axis), "cx", 1
        )
        relay = jnp.concatenate([relay_a, relay_b], axis=split_axis)
        return [piece, from_right, relay, from_left]
    return [piece] + [shifted(piece, "cx", -d) for d in range(1, nx)]


def shards(inner_gate, outer_gate, signal, filters, bypass, query_rows, key_rows):
    local_rows, channels = signal.shape
    nz = lax.axis_size("cz")
    nx = lax.axis_size("cx")
    members = nz * nx
    heads = channels // DH
    my_x = lax.axis_index("cx")

    product = (inner_gate.astype(jnp.float32) * signal.astype(jnp.float32)).astype(jnp.bfloat16)
    left_rim = lax.ppermute(
        product[local_rows - (TAPS - 1) :],
        ("cz", "cx"),
        [(i, i + 1) for i in range(members - 1)],
    )
    extended = jnp.concatenate(
        [left_rim, product, jnp.zeros((1, channels), jnp.bfloat16)], axis=0
    )
    hyena_out, v_heads = hyena_local(extended, filters, outer_gate, bypass, TAPS)

    def by_head(a):
        return a.reshape(local_rows, heads, DH).transpose(1, 0, 2)

    qkv = jnp.stack([by_head(query_rows), by_head(key_rows), v_heads], axis=1)
    spread = lax.all_to_all(qkv, "cz", 0, 0, tiled=True)
    q_here = spread[:, 0]
    got = gather_x(spread[:, 1:].transpose(1, 0, 2, 3), nx, 1)
    ks = [g[0] for g in got]
    vs = [g[1] for g in got]
    x_index = jnp.reshape(my_x, (1,)).astype(jnp.int32)
    out_here = attend_local(x_index, q_here, ks, vs, nx)
    returned = lax.all_to_all(out_here, "cz", 0, 0, tiled=True)
    attended = returned.transpose(1, 0, 2).reshape(local_rows, channels)
    return (hyena_out, attended)


def ctx_split(mesh):
    devices = np.asarray(mesh.devices)
    row = devices[0]
    try:
        nx = len({d.coords[0] for d in row})
    except Exception:
        nx = 4
    if row.size % nx:
        nx = 1
    return Mesh(devices.reshape(devices.shape[0], row.size // nx, nx), ("dp", "cz", "cx"))


def solution(mesh):
    split = ctx_split(mesh)
    rows = P(("dp", "cz", "cx"), None)
    placed = (rows, rows, rows, P(), P(), rows, rows)
    return jax.shard_map(
        shards,
        mesh=split,
        in_specs=placed,
        out_specs=(rows, rows),
        check_vma=False,
    )
```

```python
import math

import numpy as np
import jax
import jax.numpy as jnp
from jax import lax
from jax.sharding import Mesh, PartitionSpec as P
from jax.experimental import pallas as pl
from jax.experimental.pallas import tpu as pltpu

DH = 128
TAPS = 128


def shifted(array, axis, by):
    n = lax.axis_size(axis)
    return lax.ppermute(array, axis, [(i, (i + by) % n) for i in range(n)])


def band_dots(x, q_ref, k, mask, lane_group, rows, groups_per_chunk):
    acc = jnp.zeros((rows, 128), jnp.float32)
    for gg in range(groups_per_chunk):
        g = k * groups_per_chunk + gg
        row = q_ref[pl.ds(g, 1), :]
        rolled = pltpu.roll(jnp.broadcast_to(row, (rows, rows)), 0, 1, stride=1, stride_axis=0)
        band = jnp.where(mask, rolled, 0.0)
        hi = band.astype(jnp.bfloat16)
        lo = (band - hi.astype(jnp.float32)).astype(jnp.bfloat16)
        y = jnp.dot(hi, x, preferred_element_type=jnp.float32) + jnp.dot(
            lo, x, preferred_element_type=jnp.float32
        )
        acc = jnp.where(lane_group == gg, y, acc)
    return acc


def conv_own_kernel(cur_ref, q_ref, part_ref, *, group_width):
    rows, channels = cur_ref.shape
    groups_per_chunk = 128 // group_width
    lane_group = lax.broadcasted_iota(jnp.int32, (rows, 128), 1) // group_width
    t = lax.broadcasted_iota(jnp.int32, (rows, rows), 0)
    r = lax.broadcasted_iota(jnp.int32, (rows, rows), 1)
    lower = r <= t

    def chunk(k, carry):
        col = pl.multiple_of(k * 128, 128)
        x = cur_ref[:, pl.ds(col, 128)]
        part_ref[:, pl.ds(col, 128)] = band_dots(
            x, q_ref, k, lower, lane_group, rows, groups_per_chunk
        )
        return carry

    lax.fori_loop(0, channels // 128, chunk, 0)


def conv_rim_kernel(prev_ref, cur_ref, q_ref, part_ref, outer_ref, bypass_ref, out_ref, heads_ref, *, group_width):
    rows, channels = cur_ref.shape
    groups_per_chunk = 128 // group_width
    lane_group = lax.broadcasted_iota(jnp.int32, (rows, 128), 1) // group_width
    t = lax.broadcasted_iota(jnp.int32, (rows, rows), 0)
    r = lax.broadcasted_iota(jnp.int32, (rows, rows), 1)
    upper = r > t

    def chunk(k, carry):
        col = pl.multiple_of(k * 128, 128)
        x = prev_ref[:, pl.ds(col, 128)]
        acc = band_dots(x, q_ref, k, upper, lane_group, rows, groups_per_chunk)
        acc = acc + part_ref[:, pl.ds(col, 128)]
        product = cur_ref[:, pl.ds(col, 128)].astype(jnp.float32)
        outer = outer_ref[:, pl.ds(col, 128)].astype(jnp.float32)
        bypass = bypass_ref[:, pl.ds(col, 128)]
        result = (outer * (acc + bypass * product)).astype(out_ref.dtype)
        out_ref[:, pl.ds(col, 128)] = result
        heads_ref[k] = result
        return carry

    lax.fori_loop(0, channels // 128, chunk, 0)


def hyena_local(prev, cur, filters, outer, bypass):
    rows, channels = outer.shape
    group_count, taps = filters.shape
    rotated = jnp.roll(filters[:, ::-1], 1, axis=1)
    width = channels // group_count
    vmem = pl.BlockSpec(memory_space=pltpu.VMEM)
    flops = 2 * 2 * 8 * rows * rows * channels
    part = pl.pallas_call(
        lambda *refs: conv_own_kernel(*refs, group_width=width),
        out_shape=jax.ShapeDtypeStruct((rows, channels), jnp.float32),
        in_specs=[vmem] * 2,
        out_specs=vmem,
        cost_estimate=pl.CostEstimate(
            flops=flops, transcendentals=0, bytes_accessed=2 * cur.size + 4 * cur.size
        ),
    )(cur, rotated)
    return pl.pallas_call(
        lambda *refs: conv_rim_kernel(*refs, group_width=width),
        out_shape=(
            jax.ShapeDtypeStruct((rows, channels), jnp.bfloat16),
            jax.ShapeDtypeStruct((channels // DH, rows, DH), jnp.bfloat16),
        ),
        in_specs=[vmem] * 6,
        out_specs=(vmem, vmem),
        cost_estimate=pl.CostEstimate(
            flops=flops, transcendentals=0, bytes_accessed=16 * cur.size
        ),
    )(prev, cur, rotated, part, outer, bypass.reshape(1, channels))


def attend_kernel(x_ref, q_ref, *refs, nx):
    k_refs = refs[:nx]
    v_refs = refs[nx : 2 * nx]
    o_ref = refs[2 * nx]
    x = x_ref[0]
    blocks, rows, dh = q_ref.shape
    inv_root = 1.0 / math.sqrt(DH)
    for i in range(blocks):
        length = (i + 1) * rows
        q = q_ref[i]
        qpos = (i * nx + x) * rows + lax.broadcasted_iota(jnp.int32, (rows, length), 0)
        col = lax.broadcasted_iota(jnp.int32, (rows, length), 1)
        pieces = []
        for d in range(nx):
            xd = lax.rem(x + d, nx)
            k = k_refs[d][: i + 1].reshape(length, dh)
            s = lax.dot_general(
                q, k, (((1,), (1,)), ((), ())), preferred_element_type=jnp.float32
            ) * inv_root
            kpos = ((col // rows) * nx + xd) * rows + lax.rem(col, rows)
            visible = kpos <= qpos
            pieces.append((jnp.where(visible, s, -1e30), visible))
        highest = jnp.max(pieces[0][0], axis=1, keepdims=True)
        for s, _ in pieces[1:]:
            highest = jnp.maximum(highest, jnp.max(s, axis=1, keepdims=True))
        total = None
        acc = None
        for d, (s, visible) in enumerate(pieces):
            w = jnp.where(visible, jnp.exp(s - highest), 0.0)
            part_sum = jnp.sum(w, axis=1, keepdims=True)
            v = v_refs[d][: i + 1].reshape(length, dh)
            part = jnp.dot(w.astype(jnp.bfloat16), v, preferred_element_type=jnp.float32)
            total = part_sum if total is None else total + part_sum
            acc = part if acc is None else acc + part
        o_ref[i] = (acc / total).astype(o_ref.dtype)


def attend_local(x_index, q, ks, vs, nx):
    blocks, rows, dh = q.shape
    seq = nx * blocks * rows
    flops = 2 * 2 * blocks * rows * seq * dh // 2
    vmem = pl.BlockSpec(memory_space=pltpu.VMEM)
    return pl.pallas_call(
        lambda *refs: attend_kernel(*refs, nx=nx),
        out_shape=jax.ShapeDtypeStruct(q.shape, jnp.bfloat16),
        in_specs=[pl.BlockSpec(memory_space=pltpu.SMEM)] + [vmem] * (1 + 2 * nx),
        out_specs=vmem,
        compiler_params=pltpu.CompilerParams(vmem_limit_bytes=48 * 1024 * 1024),
        cost_estimate=pl.CostEstimate(
            flops=flops,
            transcendentals=blocks * rows * seq // 2,
            bytes_accessed=2 * (2 * q.size + 2 * seq * dh),
        ),
    )(x_index, q, *ks, *vs)


def gather_x(piece, nx, split_axis=0):
    if nx == 4:
        half = piece.shape[split_axis] // 2
        from_left = shifted(piece, "cx", 1)
        from_right = shifted(piece, "cx", -1)
        relay_a = shifted(lax.slice_in_dim(from_right, 0, half, axis=split_axis), "cx", -1)
        relay_b = shifted(
            lax.slice_in_dim(from_left, half, piece.shape[split_axis], axis=split_axis), "cx", 1
        )
        relay = jnp.concatenate([relay_a, relay_b], axis=split_axis)
        return [piece, from_right, relay, from_left]
    return [piece] + [shifted(piece, "cx", -d) for d in range(1, nx)]


def shards(inner_gate, outer_gate, signal, filters, bypass, query_rows, key_rows):
    local_rows, channels = signal.shape
    nz = lax.axis_size("cz")
    nx = lax.axis_size("cx")
    members = nz * nx
    heads = channels // DH
    my_x = lax.axis_index("cx")

    product = (inner_gate.astype(jnp.float32) * signal.astype(jnp.float32)).astype(jnp.bfloat16)
    previous = lax.ppermute(
        product,
        ("cz", "cx"),
        [(i, i + 1) for i in range(members - 1)],
    )
    hyena_out, v_heads = hyena_local(previous, product, filters, outer_gate, bypass)

    def by_head(a):
        return a.reshape(local_rows, heads, DH).transpose(1, 0, 2)

    qkv = jnp.stack([by_head(query_rows), by_head(key_rows), v_heads], axis=1)
    spread = lax.all_to_all(qkv, "cz", 0, 0, tiled=True)
    q_here = spread[:, 0]
    got = gather_x(spread[:, 1:].transpose(1, 0, 2, 3), nx, 1)
    ks = [g[0] for g in got]
    vs = [g[1] for g in got]
    x_index = jnp.reshape(my_x, (1,)).astype(jnp.int32)
    out_here = attend_local(x_index, q_here, ks, vs, nx)
    returned = lax.all_to_all(out_here, "cz", 0, 0, tiled=True)
    attended = returned.transpose(1, 0, 2).reshape(local_rows, channels)
    return (hyena_out, attended)


def ctx_split(mesh):
    devices = np.asarray(mesh.devices)
    row = devices[0]
    try:
        nx = len({d.coords[0] for d in row})
    except Exception:
        nx = 4
    if row.size % nx:
        nx = 1
    return Mesh(devices.reshape(devices.shape[0], row.size // nx, nx), ("dp", "cz", "cx"))


def solution(mesh):
    split = ctx_split(mesh)
    rows = P(("dp", "cz", "cx"), None)
    placed = (rows, rows, rows, P(), P(), rows, rows)
    return jax.shard_map(
        shards,
        mesh=split,
        in_specs=placed,
        out_specs=(rows, rows),
        check_vma=False,
    )
```

```python
import math

import numpy as np
import jax
import jax.numpy as jnp
from jax import lax
from jax.sharding import Mesh, PartitionSpec as P
from jax.experimental import pallas as pl
from jax.experimental.pallas import tpu as pltpu

DH = 128
TAPS = 128


def shifted(array, axis, by):
    n = lax.axis_size(axis)
    return lax.ppermute(array, axis, [(i, (i + by) % n) for i in range(n)])


def band_dots(x, q_ref, k, mask, lane_group, rows, groups_per_chunk):
    acc = jnp.zeros((rows, 128), jnp.float32)
    for gg in range(groups_per_chunk):
        g = k * groups_per_chunk + gg
        row = q_ref[pl.ds(g, 1), :]
        rolled = pltpu.roll(jnp.broadcast_to(row, (rows, rows)), 0, 1, stride=1, stride_axis=0)
        band = jnp.where(mask, rolled, 0.0)
        hi = band.astype(jnp.bfloat16)
        lo = (band - hi.astype(jnp.float32)).astype(jnp.bfloat16)
        y = jnp.dot(hi, x, preferred_element_type=jnp.float32) + jnp.dot(
            lo, x, preferred_element_type=jnp.float32
        )
        acc = jnp.where(lane_group == gg, y, acc)
    return acc


def conv_own_kernel(cur_ref, q_ref, part_ref, *, group_width):
    rows, channels = cur_ref.shape
    groups_per_chunk = 128 // group_width
    lane_group = lax.broadcasted_iota(jnp.int32, (rows, 128), 1) // group_width
    t = lax.broadcasted_iota(jnp.int32, (rows, rows), 0)
    r = lax.broadcasted_iota(jnp.int32, (rows, rows), 1)
    lower = r <= t

    def chunk(k, carry):
        col = pl.multiple_of(k * 128, 128)
        x = cur_ref[:, pl.ds(col, 128)]
        part_ref[:, pl.ds(col, 128)] = band_dots(
            x, q_ref, k, lower, lane_group, rows, groups_per_chunk
        )
        return carry

    lax.fori_loop(0, channels // 128, chunk, 0)


def conv_rim_kernel(prev_ref, cur_ref, q_ref, part_ref, outer_ref, bypass_ref, out_ref, heads_ref, *, group_width):
    rows, channels = cur_ref.shape
    groups_per_chunk = 128 // group_width
    lane_group = lax.broadcasted_iota(jnp.int32, (rows, 128), 1) // group_width
    t = lax.broadcasted_iota(jnp.int32, (rows, rows), 0)
    r = lax.broadcasted_iota(jnp.int32, (rows, rows), 1)
    upper = r > t

    def chunk(k, carry):
        col = pl.multiple_of(k * 128, 128)
        x = prev_ref[:, pl.ds(col, 128)]
        acc = band_dots(x, q_ref, k, upper, lane_group, rows, groups_per_chunk)
        acc = acc + part_ref[:, pl.ds(col, 128)]
        product = cur_ref[:, pl.ds(col, 128)].astype(jnp.float32)
        outer = outer_ref[:, pl.ds(col, 128)].astype(jnp.float32)
        bypass = bypass_ref[:, pl.ds(col, 128)]
        result = (outer * (acc + bypass * product)).astype(out_ref.dtype)
        out_ref[:, pl.ds(col, 128)] = result
        heads_ref[k] = result
        return carry

    lax.fori_loop(0, channels // 128, chunk, 0)


def hyena_local(prev, cur, filters, outer, bypass):
    rows, channels = outer.shape
    group_count, taps = filters.shape
    rotated = jnp.roll(filters[:, ::-1], 1, axis=1)
    width = channels // group_count
    vmem = pl.BlockSpec(memory_space=pltpu.VMEM)
    flops = 2 * 2 * 8 * rows * rows * channels
    part = pl.pallas_call(
        lambda *refs: conv_own_kernel(*refs, group_width=width),
        out_shape=jax.ShapeDtypeStruct((rows, channels), jnp.float32),
        in_specs=[vmem] * 2,
        out_specs=vmem,
        cost_estimate=pl.CostEstimate(
            flops=flops, transcendentals=0, bytes_accessed=2 * cur.size + 4 * cur.size
        ),
    )(cur, rotated)
    return pl.pallas_call(
        lambda *refs: conv_rim_kernel(*refs, group_width=width),
        out_shape=(
            jax.ShapeDtypeStruct((rows, channels), jnp.bfloat16),
            jax.ShapeDtypeStruct((channels // DH, rows, DH), jnp.bfloat16),
        ),
        in_specs=[vmem] * 6,
        out_specs=(vmem, vmem),
        cost_estimate=pl.CostEstimate(
            flops=flops, transcendentals=0, bytes_accessed=16 * cur.size
        ),
    )(prev, cur, rotated, part, outer, bypass.reshape(1, channels))


def attend_kernel(x_ref, q_ref, *refs, nx):
    k_refs = refs[:nx]
    v_refs = refs[nx : 2 * nx]
    o_ref = refs[2 * nx]
    x = x_ref[0]
    blocks, rows, dh = q_ref.shape
    inv_root = 1.0 / math.sqrt(DH)
    row_id = lax.broadcasted_iota(jnp.int32, (rows, rows), 0)
    col_id = lax.broadcasted_iota(jnp.int32, (rows, rows), 1)
    for i in range(blocks):
        length = (i + 1) * rows
        q = q_ref[i]
        pieces = []
        for d in range(nx):
            xd = lax.rem(x + d, nx)
            k = k_refs[d][: i + 1].reshape(length, dh)
            s = lax.dot_general(
                q, k, (((1,), (1,)), ((), ())), preferred_element_type=jnp.float32
            ) * inv_root
            visible = (xd * rows + col_id) <= (x * rows + row_id)
            tail = jnp.where(visible, s[:, length - rows :], -1e30)
            head = s[:, : length - rows] if i > 0 else None
            pieces.append((head, tail, visible))
        highest = None
        for head, tail, _ in pieces:
            m = jnp.max(tail, axis=1, keepdims=True)
            if head is not None:
                m = jnp.maximum(m, jnp.max(head, axis=1, keepdims=True))
            highest = m if highest is None else jnp.maximum(highest, m)
        total = None
        acc = None
        for d, (head, tail, visible) in enumerate(pieces):
            w_tail = jnp.where(visible, jnp.exp(tail - highest), 0.0)
            part_sum = jnp.sum(w_tail, axis=1, keepdims=True)
            v_tail = v_refs[d][i]
            part = jnp.dot(w_tail.astype(jnp.bfloat16), v_tail, preferred_element_type=jnp.float32)
            if head is not None:
                w_head = jnp.exp(head - highest)
                part_sum = part_sum + jnp.sum(w_head, axis=1, keepdims=True)
                v_head = v_refs[d][:i].reshape(length - rows, dh)
                part = part + jnp.dot(
                    w_head.astype(jnp.bfloat16), v_head, preferred_element_type=jnp.float32
                )
            total = part_sum if total is None else total + part_sum
            acc = part if acc is None else acc + part
        o_ref[i] = (acc / total).astype(o_ref.dtype)


def attend_local(x_index, q, ks, vs, nx):
    blocks, rows, dh = q.shape
    seq = nx * blocks * rows
    flops = 2 * 2 * blocks * rows * seq * dh // 2
    vmem = pl.BlockSpec(memory_space=pltpu.VMEM)
    return pl.pallas_call(
        lambda *refs: attend_kernel(*refs, nx=nx),
        out_shape=jax.ShapeDtypeStruct(q.shape, jnp.bfloat16),
        in_specs=[pl.BlockSpec(memory_space=pltpu.SMEM)] + [vmem] * (1 + 2 * nx),
        out_specs=vmem,
        compiler_params=pltpu.CompilerParams(vmem_limit_bytes=48 * 1024 * 1024),
        cost_estimate=pl.CostEstimate(
            flops=flops,
            transcendentals=blocks * rows * seq // 2,
            bytes_accessed=2 * (2 * q.size + 2 * seq * dh),
        ),
    )(x_index, q, *ks, *vs)


def gather_x(piece, nx, split_axis=0):
    if nx == 4:
        half = piece.shape[split_axis] // 2
        from_left = shifted(piece, "cx", 1)
        from_right = shifted(piece, "cx", -1)
        relay_a = shifted(lax.slice_in_dim(from_right, 0, half, axis=split_axis), "cx", -1)
        relay_b = shifted(
            lax.slice_in_dim(from_left, half, piece.shape[split_axis], axis=split_axis), "cx", 1
        )
        relay = jnp.concatenate([relay_a, relay_b], axis=split_axis)
        return [piece, from_right, relay, from_left]
    return [piece] + [shifted(piece, "cx", -d) for d in range(1, nx)]


def shards(inner_gate, outer_gate, signal, filters, bypass, query_rows, key_rows):
    local_rows, channels = signal.shape
    nz = lax.axis_size("cz")
    nx = lax.axis_size("cx")
    members = nz * nx
    heads = channels // DH
    my_x = lax.axis_index("cx")

    product = (inner_gate.astype(jnp.float32) * signal.astype(jnp.float32)).astype(jnp.bfloat16)
    previous = lax.ppermute(
        product,
        ("cz", "cx"),
        [(i, i + 1) for i in range(members - 1)],
    )
    hyena_out, v_heads = hyena_local(previous, product, filters, outer_gate, bypass)

    def by_head(a):
        return a.reshape(local_rows, heads, DH).transpose(1, 0, 2)

    qkv = jnp.stack([by_head(query_rows), by_head(key_rows), v_heads], axis=1)
    spread = lax.all_to_all(qkv, "cz", 0, 0, tiled=True)
    q_here = spread[:, 0]
    got = gather_x(spread[:, 1:].transpose(1, 0, 2, 3), nx, 1)
    ks = [g[0] for g in got]
    vs = [g[1] for g in got]
    x_index = jnp.reshape(my_x, (1,)).astype(jnp.int32)
    out_here = attend_local(x_index, q_here, ks, vs, nx)
    returned = lax.all_to_all(out_here, "cz", 0, 0, tiled=True)
    attended = returned.transpose(1, 0, 2).reshape(local_rows, channels)
    return (hyena_out, attended)


def ctx_split(mesh):
    devices = np.asarray(mesh.devices)
    row = devices[0]
    try:
        nx = len({d.coords[0] for d in row})
    except Exception:
        nx = 4
    if row.size % nx:
        nx = 1
    return Mesh(devices.reshape(devices.shape[0], row.size // nx, nx), ("dp", "cz", "cx"))


def solution(mesh):
    split = ctx_split(mesh)
    rows = P(("dp", "cz", "cx"), None)
    placed = (rows, rows, rows, P(), P(), rows, rows)
    return jax.shard_map(
        shards,
        mesh=split,
        in_specs=placed,
        out_specs=(rows, rows),
        check_vma=False,
    )
```

```python
import math

import numpy as np
import jax
import jax.numpy as jnp
from jax import lax
from jax.sharding import Mesh, PartitionSpec as P
from jax.experimental import pallas as pl
from jax.experimental.pallas import tpu as pltpu

DH = 128
TAPS = 128


def shifted(array, axis, by):
    n = lax.axis_size(axis)
    return lax.ppermute(array, axis, [(i, (i + by) % n) for i in range(n)])


def band_dots(x, q_ref, k, mask, lane_group, rows, groups_per_chunk):
    bands = []
    for gg in range(groups_per_chunk):
        g = k * groups_per_chunk + gg
        row = q_ref[pl.ds(g, 1), :]
        rolled = pltpu.roll(jnp.broadcast_to(row, (rows, rows)), 0, 1, stride=1, stride_axis=0)
        bands.append(jnp.where(mask, rolled, 0.0))
    band = jnp.concatenate(bands, axis=0)
    hi = band.astype(jnp.bfloat16)
    lo = (band - hi.astype(jnp.float32)).astype(jnp.bfloat16)
    y = jnp.dot(hi, x, preferred_element_type=jnp.float32) + jnp.dot(
        lo, x, preferred_element_type=jnp.float32
    )
    acc = y[:rows]
    for gg in range(1, groups_per_chunk):
        acc = jnp.where(lane_group == gg, y[gg * rows : (gg + 1) * rows], acc)
    return acc


def conv_own_kernel(cur_ref, q_ref, part_ref, *, group_width):
    rows, channels = cur_ref.shape
    groups_per_chunk = 128 // group_width
    lane_group = lax.broadcasted_iota(jnp.int32, (rows, 128), 1) // group_width
    t = lax.broadcasted_iota(jnp.int32, (rows, rows), 0)
    r = lax.broadcasted_iota(jnp.int32, (rows, rows), 1)
    lower = r <= t

    def chunk(k, carry):
        col = pl.multiple_of(k * 128, 128)
        x = cur_ref[:, pl.ds(col, 128)]
        part_ref[:, pl.ds(col, 128)] = band_dots(
            x, q_ref, k, lower, lane_group, rows, groups_per_chunk
        )
        return carry

    lax.fori_loop(0, channels // 128, chunk, 0)


def conv_rim_kernel(prev_ref, cur_ref, q_ref, part_ref, outer_ref, bypass_ref, out_ref, heads_ref, *, group_width):
    rows, channels = cur_ref.shape
    groups_per_chunk = 128 // group_width
    lane_group = lax.broadcasted_iota(jnp.int32, (rows, 128), 1) // group_width
    t = lax.broadcasted_iota(jnp.int32, (rows, rows), 0)
    r = lax.broadcasted_iota(jnp.int32, (rows, rows), 1)
    upper = r > t

    def chunk(k, carry):
        col = pl.multiple_of(k * 128, 128)
        x = prev_ref[:, pl.ds(col, 128)]
        acc = band_dots(x, q_ref, k, upper, lane_group, rows, groups_per_chunk)
        acc = acc + part_ref[:, pl.ds(col, 128)]
        product = cur_ref[:, pl.ds(col, 128)].astype(jnp.float32)
        outer = outer_ref[:, pl.ds(col, 128)].astype(jnp.float32)
        bypass = bypass_ref[:, pl.ds(col, 128)]
        result = (outer * (acc + bypass * product)).astype(out_ref.dtype)
        out_ref[:, pl.ds(col, 128)] = result
        heads_ref[k] = result
        return carry

    lax.fori_loop(0, channels // 128, chunk, 0)


def hyena_local(prev, cur, filters, outer, bypass):
    rows, channels = outer.shape
    group_count, taps = filters.shape
    rotated = jnp.roll(filters[:, ::-1], 1, axis=1)
    width = channels // group_count
    vmem = pl.BlockSpec(memory_space=pltpu.VMEM)
    flops = 2 * 2 * 8 * rows * rows * channels
    part = pl.pallas_call(
        lambda *refs: conv_own_kernel(*refs, group_width=width),
        out_shape=jax.ShapeDtypeStruct((rows, channels), jnp.float32),
        in_specs=[vmem] * 2,
        out_specs=vmem,
        cost_estimate=pl.CostEstimate(
            flops=flops, transcendentals=0, bytes_accessed=2 * cur.size + 4 * cur.size
        ),
    )(cur, rotated)
    return pl.pallas_call(
        lambda *refs: conv_rim_kernel(*refs, group_width=width),
        out_shape=(
            jax.ShapeDtypeStruct((rows, channels), jnp.bfloat16),
            jax.ShapeDtypeStruct((channels // DH, rows, DH), jnp.bfloat16),
        ),
        in_specs=[vmem] * 6,
        out_specs=(vmem, vmem),
        cost_estimate=pl.CostEstimate(
            flops=flops, transcendentals=0, bytes_accessed=16 * cur.size
        ),
    )(prev, cur, rotated, part, outer, bypass.reshape(1, channels))


def attend_kernel(x_ref, q_ref, *refs, nx):
    k_refs = refs[:nx]
    v_refs = refs[nx : 2 * nx]
    o_ref = refs[2 * nx]
    x = x_ref[0]
    blocks, rows, dh = q_ref.shape
    inv_root = 1.0 / math.sqrt(DH)
    row_id = lax.broadcasted_iota(jnp.int32, (rows, rows), 0)
    col_id = lax.broadcasted_iota(jnp.int32, (rows, rows), 1)
    for i in range(blocks):
        length = (i + 1) * rows
        q = q_ref[i]
        pieces = []
        for d in range(nx):
            xd = lax.rem(x + d, nx)
            k = k_refs[d][: i + 1].reshape(length, dh)
            s = lax.dot_general(
                q, k, (((1,), (1,)), ((), ())), preferred_element_type=jnp.float32
            ) * inv_root
            visible = (xd * rows + col_id) <= (x * rows + row_id)
            tail = jnp.where(visible, s[:, length - rows :], -1e30)
            head = s[:, : length - rows] if i > 0 else None
            pieces.append((head, tail, visible))
        highest = None
        for head, tail, _ in pieces:
            m = jnp.max(tail, axis=1, keepdims=True)
            if head is not None:
                m = jnp.maximum(m, jnp.max(head, axis=1, keepdims=True))
            highest = m if highest is None else jnp.maximum(highest, m)
        total = None
        acc = None
        for d, (head, tail, visible) in enumerate(pieces):
            w_tail = jnp.where(visible, jnp.exp(tail - highest), 0.0)
            part_sum = jnp.sum(w_tail, axis=1, keepdims=True)
            v_tail = v_refs[d][i]
            part = jnp.dot(w_tail.astype(jnp.bfloat16), v_tail, preferred_element_type=jnp.float32)
            if head is not None:
                w_head = jnp.exp(head - highest)
                part_sum = part_sum + jnp.sum(w_head, axis=1, keepdims=True)
                v_head = v_refs[d][:i].reshape(length - rows, dh)
                part = part + jnp.dot(
                    w_head.astype(jnp.bfloat16), v_head, preferred_element_type=jnp.float32
                )
            total = part_sum if total is None else total + part_sum
            acc = part if acc is None else acc + part
        o_ref[i] = (acc / total).astype(o_ref.dtype)


def attend_local(x_index, q, ks, vs, nx):
    blocks, rows, dh = q.shape
    seq = nx * blocks * rows
    flops = 2 * 2 * blocks * rows * seq * dh // 2
    vmem = pl.BlockSpec(memory_space=pltpu.VMEM)
    return pl.pallas_call(
        lambda *refs: attend_kernel(*refs, nx=nx),
        out_shape=jax.ShapeDtypeStruct(q.shape, jnp.bfloat16),
        in_specs=[pl.BlockSpec(memory_space=pltpu.SMEM)] + [vmem] * (1 + 2 * nx),
        out_specs=vmem,
        compiler_params=pltpu.CompilerParams(vmem_limit_bytes=48 * 1024 * 1024),
        cost_estimate=pl.CostEstimate(
            flops=flops,
            transcendentals=blocks * rows * seq // 2,
            bytes_accessed=2 * (2 * q.size + 2 * seq * dh),
        ),
    )(x_index, q, *ks, *vs)


def gather_x(piece, nx, split_axis=0):
    if nx == 4:
        half = piece.shape[split_axis] // 2
        from_left = shifted(piece, "cx", 1)
        from_right = shifted(piece, "cx", -1)
        relay_a = shifted(lax.slice_in_dim(from_right, 0, half, axis=split_axis), "cx", -1)
        relay_b = shifted(
            lax.slice_in_dim(from_left, half, piece.shape[split_axis], axis=split_axis), "cx", 1
        )
        relay = jnp.concatenate([relay_a, relay_b], axis=split_axis)
        return [piece, from_right, relay, from_left]
    return [piece] + [shifted(piece, "cx", -d) for d in range(1, nx)]


def shards(inner_gate, outer_gate, signal, filters, bypass, query_rows, key_rows):
    local_rows, channels = signal.shape
    nz = lax.axis_size("cz")
    nx = lax.axis_size("cx")
    members = nz * nx
    heads = channels // DH
    my_x = lax.axis_index("cx")

    product = (inner_gate.astype(jnp.float32) * signal.astype(jnp.float32)).astype(jnp.bfloat16)
    previous = lax.ppermute(
        product,
        ("cz", "cx"),
        [(i, i + 1) for i in range(members - 1)],
    )
    hyena_out, v_heads = hyena_local(previous, product, filters, outer_gate, bypass)

    def by_head(a):
        return a.reshape(local_rows, heads, DH).transpose(1, 0, 2)

    qkv = jnp.stack([by_head(query_rows), by_head(key_rows), v_heads], axis=1)
    spread = lax.all_to_all(qkv, "cz", 0, 0, tiled=True)
    q_here = spread[:, 0]
    got = gather_x(spread[:, 1:].transpose(1, 0, 2, 3), nx, 1)
    ks = [g[0] for g in got]
    vs = [g[1] for g in got]
    x_index = jnp.reshape(my_x, (1,)).astype(jnp.int32)
    out_here = attend_local(x_index, q_here, ks, vs, nx)
    returned = lax.all_to_all(out_here, "cz", 0, 0, tiled=True)
    attended = returned.transpose(1, 0, 2).reshape(local_rows, channels)
    return (hyena_out, attended)


def ctx_split(mesh):
    devices = np.asarray(mesh.devices)
    row = devices[0]
    try:
        nx = len({d.coords[0] for d in row})
    except Exception:
        nx = 4
    if row.size % nx:
        nx = 1
    return Mesh(devices.reshape(devices.shape[0], row.size // nx, nx), ("dp", "cz", "cx"))


def solution(mesh):
    split = ctx_split(mesh)
    rows = P(("dp", "cz", "cx"), None)
    placed = (rows, rows, rows, P(), P(), rows, rows)
    return jax.shard_map(
        shards,
        mesh=split,
        in_specs=placed,
        out_specs=(rows, rows),
        check_vma=False,
    )
```

```python
import math

import numpy as np
import jax
import jax.numpy as jnp
from jax import lax
from jax.sharding import Mesh, PartitionSpec as P
from jax.experimental import pallas as pl
from jax.experimental.pallas import tpu as pltpu

DH = 128
TAPS = 128


def shifted(array, axis, by):
    n = lax.axis_size(axis)
    return lax.ppermute(array, axis, [(i, (i + by) % n) for i in range(n)])


def band_dots(x, q_ref, k, mask, lane_group, rows, groups_per_chunk):
    bands = []
    for gg in range(groups_per_chunk):
        g = k * groups_per_chunk + gg
        row = q_ref[pl.ds(g, 1), :]
        rolled = pltpu.roll(jnp.broadcast_to(row, (rows, rows)), 0, 1, stride=1, stride_axis=0)
        bands.append(jnp.where(mask, rolled, 0.0))
    band = jnp.concatenate(bands, axis=0)
    hi = band.astype(jnp.bfloat16)
    lo = (band - hi.astype(jnp.float32)).astype(jnp.bfloat16)
    y = jnp.dot(hi, x, preferred_element_type=jnp.float32) + jnp.dot(
        lo, x, preferred_element_type=jnp.float32
    )
    acc = y[:rows]
    for gg in range(1, groups_per_chunk):
        acc = jnp.where(lane_group == gg, y[gg * rows : (gg + 1) * rows], acc)
    return acc


def conv_own_kernel(cur_ref, q_ref, part_ref, *, group_width):
    rows, channels = cur_ref.shape
    groups_per_chunk = 128 // group_width
    lane_group = lax.broadcasted_iota(jnp.int32, (rows, 128), 1) // group_width
    t = lax.broadcasted_iota(jnp.int32, (rows, rows), 0)
    r = lax.broadcasted_iota(jnp.int32, (rows, rows), 1)
    lower = r <= t

    def chunk(k, carry):
        col = pl.multiple_of(k * 128, 128)
        x = cur_ref[:, pl.ds(col, 128)]
        part_ref[:, pl.ds(col, 128)] = band_dots(
            x, q_ref, k, lower, lane_group, rows, groups_per_chunk
        )
        return carry

    lax.fori_loop(0, channels // 128, chunk, 0)


def conv_rim_kernel(prev_ref, cur_ref, q_ref, part_ref, outer_ref, bypass_ref, query_ref, key_ref, out_ref, heads_ref, *, group_width):
    rows, channels = cur_ref.shape
    groups_per_chunk = 128 // group_width
    lane_group = lax.broadcasted_iota(jnp.int32, (rows, 128), 1) // group_width
    t = lax.broadcasted_iota(jnp.int32, (rows, rows), 0)
    r = lax.broadcasted_iota(jnp.int32, (rows, rows), 1)
    upper = r > t

    def chunk(k, carry):
        col = pl.multiple_of(k * 128, 128)
        x = prev_ref[:, pl.ds(col, 128)]
        acc = band_dots(x, q_ref, k, upper, lane_group, rows, groups_per_chunk)
        acc = acc + part_ref[:, pl.ds(col, 128)]
        product = cur_ref[:, pl.ds(col, 128)].astype(jnp.float32)
        outer = outer_ref[:, pl.ds(col, 128)].astype(jnp.float32)
        bypass = bypass_ref[:, pl.ds(col, 128)]
        result = (outer * (acc + bypass * product)).astype(out_ref.dtype)
        out_ref[:, pl.ds(col, 128)] = result
        heads_ref[k, 0] = query_ref[:, pl.ds(col, 128)]
        heads_ref[k, 1] = key_ref[:, pl.ds(col, 128)]
        heads_ref[k, 2] = result
        return carry

    lax.fori_loop(0, channels // 128, chunk, 0)


def hyena_local(prev, cur, filters, outer, bypass, query_rows, key_rows):
    rows, channels = outer.shape
    group_count, taps = filters.shape
    rotated = jnp.roll(filters[:, ::-1], 1, axis=1)
    width = channels // group_count
    vmem = pl.BlockSpec(memory_space=pltpu.VMEM)
    flops = 2 * 2 * 8 * rows * rows * channels
    part = pl.pallas_call(
        lambda *refs: conv_own_kernel(*refs, group_width=width),
        out_shape=jax.ShapeDtypeStruct((rows, channels), jnp.float32),
        in_specs=[vmem] * 2,
        out_specs=vmem,
        cost_estimate=pl.CostEstimate(
            flops=flops, transcendentals=0, bytes_accessed=2 * cur.size + 4 * cur.size
        ),
    )(cur, rotated)
    return pl.pallas_call(
        lambda *refs: conv_rim_kernel(*refs, group_width=width),
        out_shape=(
            jax.ShapeDtypeStruct((rows, channels), jnp.bfloat16),
            jax.ShapeDtypeStruct((channels // DH, 3, rows, DH), jnp.bfloat16),
        ),
        in_specs=[vmem] * 8,
        out_specs=(vmem, vmem),
        cost_estimate=pl.CostEstimate(
            flops=flops, transcendentals=0, bytes_accessed=16 * cur.size
        ),
    )(prev, cur, rotated, part, outer, bypass.reshape(1, channels), query_rows, key_rows)


def attend_kernel(x_ref, q_ref, *refs, nx):
    k_refs = refs[:nx]
    v_refs = refs[nx : 2 * nx]
    o_ref = refs[2 * nx]
    x = x_ref[0]
    blocks, rows, dh = q_ref.shape
    inv_root = 1.0 / math.sqrt(DH)
    row_id = lax.broadcasted_iota(jnp.int32, (rows, rows), 0)
    col_id = lax.broadcasted_iota(jnp.int32, (rows, rows), 1)
    for i in range(blocks):
        length = (i + 1) * rows
        q = q_ref[i]
        pieces = []
        for d in range(nx):
            xd = lax.rem(x + d, nx)
            k = k_refs[d][: i + 1].reshape(length, dh)
            s = lax.dot_general(
                q, k, (((1,), (1,)), ((), ())), preferred_element_type=jnp.float32
            ) * inv_root
            visible = (xd * rows + col_id) <= (x * rows + row_id)
            tail = jnp.where(visible, s[:, length - rows :], -1e30)
            head = s[:, : length - rows] if i > 0 else None
            pieces.append((head, tail, visible))
        highest = None
        for head, tail, _ in pieces:
            m = jnp.max(tail, axis=1, keepdims=True)
            if head is not None:
                m = jnp.maximum(m, jnp.max(head, axis=1, keepdims=True))
            highest = m if highest is None else jnp.maximum(highest, m)
        total = None
        acc = None
        for d, (head, tail, visible) in enumerate(pieces):
            w_tail = jnp.where(visible, jnp.exp(tail - highest), 0.0)
            part_sum = jnp.sum(w_tail, axis=1, keepdims=True)
            v_tail = v_refs[d][i]
            part = jnp.dot(w_tail.astype(jnp.bfloat16), v_tail, preferred_element_type=jnp.float32)
            if head is not None:
                w_head = jnp.exp(head - highest)
                part_sum = part_sum + jnp.sum(w_head, axis=1, keepdims=True)
                v_head = v_refs[d][:i].reshape(length - rows, dh)
                part = part + jnp.dot(
                    w_head.astype(jnp.bfloat16), v_head, preferred_element_type=jnp.float32
                )
            total = part_sum if total is None else total + part_sum
            acc = part if acc is None else acc + part
        o_ref[i] = (acc / total).astype(o_ref.dtype)


def attend_local(x_index, q, ks, vs, nx):
    blocks, rows, dh = q.shape
    seq = nx * blocks * rows
    flops = 2 * 2 * blocks * rows * seq * dh // 2
    vmem = pl.BlockSpec(memory_space=pltpu.VMEM)
    return pl.pallas_call(
        lambda *refs: attend_kernel(*refs, nx=nx),
        out_shape=jax.ShapeDtypeStruct(q.shape, jnp.bfloat16),
        in_specs=[pl.BlockSpec(memory_space=pltpu.SMEM)] + [vmem] * (1 + 2 * nx),
        out_specs=vmem,
        compiler_params=pltpu.CompilerParams(vmem_limit_bytes=48 * 1024 * 1024),
        cost_estimate=pl.CostEstimate(
            flops=flops,
            transcendentals=blocks * rows * seq // 2,
            bytes_accessed=2 * (2 * q.size + 2 * seq * dh),
        ),
    )(x_index, q, *ks, *vs)


def gather_x(piece, nx, split_axis=0):
    if nx == 4:
        half = piece.shape[split_axis] // 2
        from_left = shifted(piece, "cx", 1)
        from_right = shifted(piece, "cx", -1)
        relay_a = shifted(lax.slice_in_dim(from_right, 0, half, axis=split_axis), "cx", -1)
        relay_b = shifted(
            lax.slice_in_dim(from_left, half, piece.shape[split_axis], axis=split_axis), "cx", 1
        )
        relay = jnp.concatenate([relay_a, relay_b], axis=split_axis)
        return [piece, from_right, relay, from_left]
    return [piece] + [shifted(piece, "cx", -d) for d in range(1, nx)]


def shards(inner_gate, outer_gate, signal, filters, bypass, query_rows, key_rows):
    local_rows, channels = signal.shape
    nz = lax.axis_size("cz")
    nx = lax.axis_size("cx")
    members = nz * nx
    heads = channels // DH
    my_x = lax.axis_index("cx")

    product = (inner_gate.astype(jnp.float32) * signal.astype(jnp.float32)).astype(jnp.bfloat16)
    previous = lax.ppermute(
        product,
        ("cz", "cx"),
        [(i, i + 1) for i in range(members - 1)],
    )
    hyena_out, qkv = hyena_local(previous, product, filters, outer_gate, bypass, query_rows, key_rows)

    spread = lax.all_to_all(qkv, "cz", 0, 0, tiled=True)
    q_here = spread[:, 0]
    got = gather_x(spread[:, 1:].transpose(1, 0, 2, 3), nx, 1)
    ks = [g[0] for g in got]
    vs = [g[1] for g in got]
    x_index = jnp.reshape(my_x, (1,)).astype(jnp.int32)
    out_here = attend_local(x_index, q_here, ks, vs, nx)
    returned = lax.all_to_all(out_here, "cz", 0, 0, tiled=True)
    attended = returned.transpose(1, 0, 2).reshape(local_rows, channels)
    return (hyena_out, attended)


def ctx_split(mesh):
    devices = np.asarray(mesh.devices)
    row = devices[0]
    try:
        nx = len({d.coords[0] for d in row})
    except Exception:
        nx = 4
    if row.size % nx:
        nx = 1
    return Mesh(devices.reshape(devices.shape[0], row.size // nx, nx), ("dp", "cz", "cx"))


def solution(mesh):
    split = ctx_split(mesh)
    rows = P(("dp", "cz", "cx"), None)
    placed = (rows, rows, rows, P(), P(), rows, rows)
    return jax.shard_map(
        shards,
        mesh=split,
        in_specs=placed,
        out_specs=(rows, rows),
        check_vma=False,
    )
```

```python
import math

import numpy as np
import jax
import jax.numpy as jnp
from jax import lax
from jax.sharding import Mesh, PartitionSpec as P
from jax.experimental import pallas as pl
from jax.experimental.pallas import tpu as pltpu

DH = 128
TAPS = 128


def shifted(array, axis, by):
    n = lax.axis_size(axis)
    return lax.ppermute(array, axis, [(i, (i + by) % n) for i in range(n)])


def band_dots(x, q_ref, k, mask, lane_group, rows, groups_per_chunk):
    bands = []
    for gg in range(groups_per_chunk):
        g = k * groups_per_chunk + gg
        row = q_ref[pl.ds(g, 1), :]
        rolled = pltpu.roll(jnp.broadcast_to(row, (rows, rows)), 0, 1, stride=1, stride_axis=0)
        bands.append(jnp.where(mask, rolled, 0.0))
    band = jnp.concatenate(bands, axis=0)
    hi = band.astype(jnp.bfloat16)
    lo = (band - hi.astype(jnp.float32)).astype(jnp.bfloat16)
    y = jnp.dot(hi, x, preferred_element_type=jnp.float32) + jnp.dot(
        lo, x, preferred_element_type=jnp.float32
    )
    acc = y[:rows]
    for gg in range(1, groups_per_chunk):
        acc = jnp.where(lane_group == gg, y[gg * rows : (gg + 1) * rows], acc)
    return acc


def conv_own_kernel(cur_ref, q_ref, part_ref, *, group_width):
    rows, channels = cur_ref.shape
    groups_per_chunk = 128 // group_width
    lane_group = lax.broadcasted_iota(jnp.int32, (rows, 128), 1) // group_width
    t = lax.broadcasted_iota(jnp.int32, (rows, rows), 0)
    r = lax.broadcasted_iota(jnp.int32, (rows, rows), 1)
    lower = r <= t

    def chunk(k, carry):
        col = pl.multiple_of(k * 128, 128)
        x = cur_ref[:, pl.ds(col, 128)]
        part_ref[:, pl.ds(col, 128)] = band_dots(
            x, q_ref, k, lower, lane_group, rows, groups_per_chunk
        )
        return carry

    lax.fori_loop(0, channels // 128, chunk, 0)


def conv_rim_kernel(prev_ref, cur_ref, q_ref, part_ref, outer_ref, bypass_ref, query_ref, key_ref, out_ref, heads_ref, *, group_width):
    rows, channels = cur_ref.shape
    groups_per_chunk = 128 // group_width
    lane_group = lax.broadcasted_iota(jnp.int32, (rows, 128), 1) // group_width
    t = lax.broadcasted_iota(jnp.int32, (rows, rows), 0)
    r = lax.broadcasted_iota(jnp.int32, (rows, rows), 1)
    upper = r > t

    def chunk(k, carry):
        col = pl.multiple_of(k * 128, 128)
        x = prev_ref[:, pl.ds(col, 128)]
        acc = band_dots(x, q_ref, k, upper, lane_group, rows, groups_per_chunk)
        acc = acc + part_ref[:, pl.ds(col, 128)]
        product = cur_ref[:, pl.ds(col, 128)].astype(jnp.float32)
        outer = outer_ref[:, pl.ds(col, 128)].astype(jnp.float32)
        bypass = bypass_ref[:, pl.ds(col, 128)]
        result = (outer * (acc + bypass * product)).astype(out_ref.dtype)
        out_ref[:, pl.ds(col, 128)] = result
        heads_ref[k, 0] = query_ref[:, pl.ds(col, 128)]
        heads_ref[k, 1] = key_ref[:, pl.ds(col, 128)]
        heads_ref[k, 2] = result
        return carry

    lax.fori_loop(0, channels // 128, chunk, 0)


def hyena_local(prev, cur, filters, outer, bypass, query_rows, key_rows):
    rows, channels = outer.shape
    group_count, taps = filters.shape
    rotated = jnp.roll(filters[:, ::-1], 1, axis=1)
    width = channels // group_count
    vmem = pl.BlockSpec(memory_space=pltpu.VMEM)
    flops = 2 * 2 * 8 * rows * rows * channels
    part = pl.pallas_call(
        lambda *refs: conv_own_kernel(*refs, group_width=width),
        out_shape=jax.ShapeDtypeStruct((rows, channels), jnp.float32),
        in_specs=[vmem] * 2,
        out_specs=vmem,
        cost_estimate=pl.CostEstimate(
            flops=flops, transcendentals=0, bytes_accessed=2 * cur.size + 4 * cur.size
        ),
    )(cur, rotated)
    return pl.pallas_call(
        lambda *refs: conv_rim_kernel(*refs, group_width=width),
        out_shape=(
            jax.ShapeDtypeStruct((rows, channels), jnp.bfloat16),
            jax.ShapeDtypeStruct((channels // DH, 3, rows, DH), jnp.bfloat16),
        ),
        in_specs=[vmem] * 8,
        out_specs=(vmem, vmem),
        cost_estimate=pl.CostEstimate(
            flops=flops, transcendentals=0, bytes_accessed=16 * cur.size
        ),
    )(prev, cur, rotated, part, outer, bypass.reshape(1, channels), query_rows, key_rows)


def piece_scores(q, k_ref, i, xd, x, rows, row_id, col_id, inv_root):
    length = (i + 1) * rows
    dh = k_ref.shape[-1]
    k = k_ref[: i + 1].reshape(length, dh)
    s = lax.dot_general(
        q, k, (((1,), (1,)), ((), ())), preferred_element_type=jnp.float32
    ) * inv_root
    visible = (xd * rows + col_id) <= (x * rows + row_id)
    tail = jnp.where(visible, s[:, length - rows :], -1e30)
    head = s[:, : length - rows] if i > 0 else None
    return head, tail, visible


def piece_max(head, tail):
    m = jnp.max(tail, axis=1, keepdims=True)
    if head is not None:
        m = jnp.maximum(m, jnp.max(head, axis=1, keepdims=True))
    return m


def piece_sums(head, tail, visible, v_ref, i, highest, rows):
    dh = v_ref.shape[-1]
    w_tail = jnp.where(visible, jnp.exp(tail - highest), 0.0)
    part_sum = jnp.sum(w_tail, axis=1, keepdims=True)
    part = jnp.dot(w_tail.astype(jnp.bfloat16), v_ref[i], preferred_element_type=jnp.float32)
    if head is not None:
        w_head = jnp.exp(head - highest)
        part_sum = part_sum + jnp.sum(w_head, axis=1, keepdims=True)
        v_head = v_ref[:i].reshape(i * rows, dh)
        part = part + jnp.dot(
            w_head.astype(jnp.bfloat16), v_head, preferred_element_type=jnp.float32
        )
    return part_sum, part


def attend_first_kernel(x_ref, q_ref, *refs, offsets, nx):
    n = len(offsets)
    k_refs = refs[:n]
    v_refs = refs[n : 2 * n]
    m_ref, l_ref, acc_ref = refs[2 * n :]
    x = x_ref[0]
    blocks, rows, dh = q_ref.shape
    inv_root = 1.0 / math.sqrt(DH)
    row_id = lax.broadcasted_iota(jnp.int32, (rows, rows), 0)
    col_id = lax.broadcasted_iota(jnp.int32, (rows, rows), 1)
    for i in range(blocks):
        q = q_ref[i]
        pieces = []
        for j, d in enumerate(offsets):
            xd = lax.rem(x + d, nx)
            pieces.append(piece_scores(q, k_refs[j], i, xd, x, rows, row_id, col_id, inv_root))
        highest = None
        for head, tail, _ in pieces:
            m = piece_max(head, tail)
            highest = m if highest is None else jnp.maximum(highest, m)
        total = None
        acc = None
        for j, (head, tail, visible) in enumerate(pieces):
            part_sum, part = piece_sums(head, tail, visible, v_refs[j], i, highest, rows)
            total = part_sum if total is None else total + part_sum
            acc = part if acc is None else acc + part
        m_ref[i] = highest
        l_ref[i] = total
        acc_ref[i] = acc


def attend_last_kernel(x_ref, q_ref, k_ref, v_ref, m_ref, l_ref, acc_ref, o_ref, *, offset, nx):
    x = x_ref[0]
    blocks, rows, dh = q_ref.shape
    inv_root = 1.0 / math.sqrt(DH)
    row_id = lax.broadcasted_iota(jnp.int32, (rows, rows), 0)
    col_id = lax.broadcasted_iota(jnp.int32, (rows, rows), 1)
    xd = lax.rem(x + offset, nx)
    for i in range(blocks):
        head, tail, visible = piece_scores(q_ref[i], k_ref, i, xd, x, rows, row_id, col_id, inv_root)
        earlier = m_ref[i]
        highest = jnp.maximum(earlier, piece_max(head, tail))
        scale = jnp.exp(earlier - highest)
        part_sum, part = piece_sums(head, tail, visible, v_ref, i, highest, rows)
        total = l_ref[i] * scale + part_sum
        acc = acc_ref[i] * scale + part
        o_ref[i] = (acc / total).astype(o_ref.dtype)


def attend_local(x_index, q, ks, vs, nx):
    blocks, rows, dh = q.shape
    seq = nx * blocks * rows
    vmem = pl.BlockSpec(memory_space=pltpu.VMEM)
    smem = pl.BlockSpec(memory_space=pltpu.SMEM)
    params = pltpu.CompilerParams(vmem_limit_bytes=48 * 1024 * 1024)
    last = 2 if nx == 4 else nx - 1
    first = [d for d in range(nx) if d != last]
    share = blocks * rows * seq * dh // nx
    m, l, acc = pl.pallas_call(
        lambda *refs: attend_first_kernel(*refs, offsets=first, nx=nx),
        out_shape=(
            jax.ShapeDtypeStruct((blocks, rows, 1), jnp.float32),
            jax.ShapeDtypeStruct((blocks, rows, 1), jnp.float32),
            jax.ShapeDtypeStruct((blocks, rows, dh), jnp.float32),
        ),
        in_specs=[smem] + [vmem] * (1 + 2 * len(first)),
        out_specs=(vmem, vmem, vmem),
        compiler_params=params,
        cost_estimate=pl.CostEstimate(
            flops=2 * share * len(first),
            transcendentals=blocks * rows * seq * len(first) // (2 * nx),
            bytes_accessed=2 * q.size + 4 * seq * dh + 4 * q.size,
        ),
    )(x_index, q, *[ks[d] for d in first], *[vs[d] for d in first])
    return pl.pallas_call(
        lambda *refs: attend_last_kernel(*refs, offset=last, nx=nx),
        out_shape=jax.ShapeDtypeStruct(q.shape, jnp.bfloat16),
        in_specs=[smem] + [vmem] * 6,
        out_specs=vmem,
        compiler_params=params,
        cost_estimate=pl.CostEstimate(
            flops=2 * share,
            transcendentals=blocks * rows * seq // (2 * nx),
            bytes_accessed=2 * q.size + seq * dh + 8 * q.size,
        ),
    )(x_index, q, ks[last], vs[last], m, l, acc)


def gather_x(piece, nx, split_axis=0):
    if nx == 4:
        half = piece.shape[split_axis] // 2
        from_left = shifted(piece, "cx", 1)
        from_right = shifted(piece, "cx", -1)
        relay_a = shifted(lax.slice_in_dim(from_right, 0, half, axis=split_axis), "cx", -1)
        relay_b = shifted(
            lax.slice_in_dim(from_left, half, piece.shape[split_axis], axis=split_axis), "cx", 1
        )
        relay = jnp.concatenate([relay_a, relay_b], axis=split_axis)
        return [piece, from_right, relay, from_left]
    return [piece] + [shifted(piece, "cx", -d) for d in range(1, nx)]


def shards(inner_gate, outer_gate, signal, filters, bypass, query_rows, key_rows):
    local_rows, channels = signal.shape
    nz = lax.axis_size("cz")
    nx = lax.axis_size("cx")
    members = nz * nx
    heads = channels // DH
    my_x = lax.axis_index("cx")

    product = (inner_gate.astype(jnp.float32) * signal.astype(jnp.float32)).astype(jnp.bfloat16)
    previous = lax.ppermute(
        product,
        ("cz", "cx"),
        [(i, i + 1) for i in range(members - 1)],
    )
    hyena_out, qkv = hyena_local(previous, product, filters, outer_gate, bypass, query_rows, key_rows)

    spread = lax.all_to_all(qkv, "cz", 0, 0, tiled=True)
    q_here = spread[:, 0]
    got = gather_x(spread[:, 1:].transpose(1, 0, 2, 3), nx, 1)
    ks = [g[0] for g in got]
    vs = [g[1] for g in got]
    x_index = jnp.reshape(my_x, (1,)).astype(jnp.int32)
    out_here = attend_local(x_index, q_here, ks, vs, nx)
    returned = lax.all_to_all(out_here, "cz", 0, 0, tiled=True)
    attended = returned.transpose(1, 0, 2).reshape(local_rows, channels)
    return (hyena_out, attended)


def ctx_split(mesh):
    devices = np.asarray(mesh.devices)
    row = devices[0]
    try:
        nx = len({d.coords[0] for d in row})
    except Exception:
        nx = 4
    if row.size % nx:
        nx = 1
    return Mesh(devices.reshape(devices.shape[0], row.size // nx, nx), ("dp", "cz", "cx"))


def solution(mesh):
    split = ctx_split(mesh)
    rows = P(("dp", "cz", "cx"), None)
    placed = (rows, rows, rows, P(), P(), rows, rows)
    return jax.shard_map(
        shards,
        mesh=split,
        in_specs=placed,
        out_specs=(rows, rows),
        check_vma=False,
    )
```

```python
import math

import numpy as np
import jax
import jax.numpy as jnp
from jax import lax
from jax.sharding import Mesh, PartitionSpec as P
from jax.experimental import pallas as pl
from jax.experimental.pallas import tpu as pltpu

DH = 128
TAPS = 128


def shifted(array, axis, by):
    n = lax.axis_size(axis)
    return lax.ppermute(array, axis, [(i, (i + by) % n) for i in range(n)])


def chunk_bands(q_ref, k, rows, groups_per_chunk):
    bands = []
    for gg in range(groups_per_chunk):
        g = k * groups_per_chunk + gg
        row = q_ref[pl.ds(g, 1), :]
        bands.append(
            pltpu.roll(jnp.broadcast_to(row, (rows, rows)), 0, 1, stride=1, stride_axis=0)
        )
    return jnp.concatenate(bands, axis=0)


def halves(band):
    hi = band.astype(jnp.bfloat16)
    lo = (band - hi.astype(jnp.float32)).astype(jnp.bfloat16)
    return hi, lo


def pick_groups(y, lane_group, rows, groups_per_chunk):
    acc = y[:rows]
    for gg in range(1, groups_per_chunk):
        acc = jnp.where(lane_group == gg, y[gg * rows : (gg + 1) * rows], acc)
    return acc


def two_dots(hi, lo, x):
    return jnp.dot(hi, x, preferred_element_type=jnp.float32) + jnp.dot(
        lo, x, preferred_element_type=jnp.float32
    )


def conv_own_kernel(cur_ref, q_ref, part_ref, up_hi_ref, up_lo_ref, *, group_width):
    rows, channels = cur_ref.shape
    groups_per_chunk = 128 // group_width
    lane_group = lax.broadcasted_iota(jnp.int32, (rows, 128), 1) // group_width
    t = lax.broadcasted_iota(jnp.int32, (groups_per_chunk * rows, rows), 0) % rows
    r = lax.broadcasted_iota(jnp.int32, (groups_per_chunk * rows, rows), 1)
    lower = r <= t

    def chunk(k, carry):
        col = pl.multiple_of(k * 128, 128)
        band = chunk_bands(q_ref, k, rows, groups_per_chunk)
        hi, lo = halves(jnp.where(lower, band, 0.0))
        x = cur_ref[:, pl.ds(col, 128)]
        part_ref[:, pl.ds(col, 128)] = pick_groups(two_dots(hi, lo, x), lane_group, rows, groups_per_chunk)
        up_hi, up_lo = halves(jnp.where(lower, 0.0, band))
        start = pl.multiple_of(k * groups_per_chunk * rows, groups_per_chunk * rows)
        up_hi_ref[pl.ds(start, groups_per_chunk * rows), :] = up_hi
        up_lo_ref[pl.ds(start, groups_per_chunk * rows), :] = up_lo
        return carry

    lax.fori_loop(0, channels // 128, chunk, 0)


def conv_rim_kernel(prev_ref, cur_ref, up_hi_ref, up_lo_ref, part_ref, outer_ref, bypass_ref, query_ref, key_ref, out_ref, heads_ref, *, group_width):
    rows, channels = cur_ref.shape
    groups_per_chunk = 128 // group_width
    lane_group = lax.broadcasted_iota(jnp.int32, (rows, 128), 1) // group_width

    def chunk(k, carry):
        col = pl.multiple_of(k * 128, 128)
        start = pl.multiple_of(k * groups_per_chunk * rows, groups_per_chunk * rows)
        hi = up_hi_ref[pl.ds(start, groups_per_chunk * rows), :]
        lo = up_lo_ref[pl.ds(start, groups_per_chunk * rows), :]
        x = prev_ref[:, pl.ds(col, 128)]
        acc = pick_groups(two_dots(hi, lo, x), lane_group, rows, groups_per_chunk)
        acc = acc + part_ref[:, pl.ds(col, 128)]
        product = cur_ref[:, pl.ds(col, 128)].astype(jnp.float32)
        outer = outer_ref[:, pl.ds(col, 128)].astype(jnp.float32)
        bypass = bypass_ref[:, pl.ds(col, 128)]
        result = (outer * (acc + bypass * product)).astype(out_ref.dtype)
        out_ref[:, pl.ds(col, 128)] = result
        heads_ref[k, 0] = query_ref[:, pl.ds(col, 128)]
        heads_ref[k, 1] = key_ref[:, pl.ds(col, 128)]
        heads_ref[k, 2] = result
        return carry

    lax.fori_loop(0, channels // 128, chunk, 0)


def hyena_local(prev, cur, filters, outer, bypass, query_rows, key_rows):
    rows, channels = outer.shape
    group_count, taps = filters.shape
    rotated = jnp.roll(filters[:, ::-1], 1, axis=1)
    width = channels // group_count
    vmem = pl.BlockSpec(memory_space=pltpu.VMEM)
    flops = 2 * 2 * 8 * rows * rows * channels
    band_shape = jax.ShapeDtypeStruct((group_count * rows, rows), jnp.bfloat16)
    part, up_hi, up_lo = pl.pallas_call(
        lambda *refs: conv_own_kernel(*refs, group_width=width),
        out_shape=(jax.ShapeDtypeStruct((rows, channels), jnp.float32), band_shape, band_shape),
        in_specs=[vmem] * 2,
        out_specs=(vmem, vmem, vmem),
        cost_estimate=pl.CostEstimate(
            flops=flops, transcendentals=0, bytes_accessed=6 * cur.size + 4 * group_count * rows * rows
        ),
    )(cur, rotated)
    return pl.pallas_call(
        lambda *refs: conv_rim_kernel(*refs, group_width=width),
        out_shape=(
            jax.ShapeDtypeStruct((rows, channels), jnp.bfloat16),
            jax.ShapeDtypeStruct((channels // DH, 3, rows, DH), jnp.bfloat16),
        ),
        in_specs=[vmem] * 9,
        out_specs=(vmem, vmem),
        cost_estimate=pl.CostEstimate(
            flops=flops, transcendentals=0, bytes_accessed=16 * cur.size + 4 * group_count * rows * rows
        ),
    )(prev, cur, up_hi, up_lo, part, outer, bypass.reshape(1, channels), query_rows, key_rows)


def piece_scores(q, k_ref, i, xd, x, rows, row_id, col_id, inv_root):
    length = (i + 1) * rows
    dh = k_ref.shape[-1]
    k = k_ref[: i + 1].reshape(length, dh)
    s = lax.dot_general(
        q, k, (((1,), (1,)), ((), ())), preferred_element_type=jnp.float32
    ) * inv_root
    visible = (xd * rows + col_id) <= (x * rows + row_id)
    tail = jnp.where(visible, s[:, length - rows :], -1e30)
    head = s[:, : length - rows] if i > 0 else None
    return head, tail, visible


def piece_max(head, tail):
    m = jnp.max(tail, axis=1, keepdims=True)
    if head is not None:
        m = jnp.maximum(m, jnp.max(head, axis=1, keepdims=True))
    return m


def piece_sums(head, tail, visible, v_ref, i, highest, rows):
    dh = v_ref.shape[-1]
    w_tail = jnp.where(visible, jnp.exp(tail - highest), 0.0)
    part_sum = jnp.sum(w_tail, axis=1, keepdims=True)
    part = jnp.dot(w_tail.astype(jnp.bfloat16), v_ref[i], preferred_element_type=jnp.float32)
    if head is not None:
        w_head = jnp.exp(head - highest)
        part_sum = part_sum + jnp.sum(w_head, axis=1, keepdims=True)
        v_head = v_ref[:i].reshape(i * rows, dh)
        part = part + jnp.dot(
            w_head.astype(jnp.bfloat16), v_head, preferred_element_type=jnp.float32
        )
    return part_sum, part


def attend_first_kernel(x_ref, q_ref, *refs, offsets, nx):
    n = len(offsets)
    k_refs = refs[:n]
    v_refs = refs[n : 2 * n]
    m_ref, l_ref, acc_ref = refs[2 * n :]
    x = x_ref[0]
    blocks, rows, dh = q_ref.shape
    inv_root = 1.0 / math.sqrt(DH)
    row_id = lax.broadcasted_iota(jnp.int32, (rows, rows), 0)
    col_id = lax.broadcasted_iota(jnp.int32, (rows, rows), 1)
    for i in range(blocks):
        q = q_ref[i]
        pieces = []
        for j, d in enumerate(offsets):
            xd = lax.rem(x + d, nx)
            pieces.append(piece_scores(q, k_refs[j], i, xd, x, rows, row_id, col_id, inv_root))
        highest = None
        for head, tail, _ in pieces:
            m = piece_max(head, tail)
            highest = m if highest is None else jnp.maximum(highest, m)
        total = None
        acc = None
        for j, (head, tail, visible) in enumerate(pieces):
            part_sum, part = piece_sums(head, tail, visible, v_refs[j], i, highest, rows)
            total = part_sum if total is None else total + part_sum
            acc = part if acc is None else acc + part
        m_ref[i] = highest
        l_ref[i] = total
        acc_ref[i] = acc


def attend_last_kernel(x_ref, q_ref, k_ref, v_ref, m_ref, l_ref, acc_ref, o_ref, *, offset, nx):
    x = x_ref[0]
    blocks, rows, dh = q_ref.shape
    inv_root = 1.0 / math.sqrt(DH)
    row_id = lax.broadcasted_iota(jnp.int32, (rows, rows), 0)
    col_id = lax.broadcasted_iota(jnp.int32, (rows, rows), 1)
    xd = lax.rem(x + offset, nx)
    for i in range(blocks):
        head, tail, visible = piece_scores(q_ref[i], k_ref, i, xd, x, rows, row_id, col_id, inv_root)
        earlier = m_ref[i]
        highest = jnp.maximum(earlier, piece_max(head, tail))
        scale = jnp.exp(earlier - highest)
        part_sum, part = piece_sums(head, tail, visible, v_ref, i, highest, rows)
        total = l_ref[i] * scale + part_sum
        acc = acc_ref[i] * scale + part
        o_ref[i] = (acc / total).astype(o_ref.dtype)


def attend_local(x_index, q, ks, vs, nx):
    blocks, rows, dh = q.shape
    seq = nx * blocks * rows
    vmem = pl.BlockSpec(memory_space=pltpu.VMEM)
    smem = pl.BlockSpec(memory_space=pltpu.SMEM)
    params = pltpu.CompilerParams(vmem_limit_bytes=48 * 1024 * 1024)
    last = 2 if nx == 4 else nx - 1
    first = [d for d in range(nx) if d != last]
    share = blocks * rows * seq * dh // nx
    m, l, acc = pl.pallas_call(
        lambda *refs: attend_first_kernel(*refs, offsets=first, nx=nx),
        out_shape=(
            jax.ShapeDtypeStruct((blocks, rows, 1), jnp.float32),
            jax.ShapeDtypeStruct((blocks, rows, 1), jnp.float32),
            jax.ShapeDtypeStruct((blocks, rows, dh), jnp.float32),
        ),
        in_specs=[smem] + [vmem] * (1 + 2 * len(first)),
        out_specs=(vmem, vmem, vmem),
        compiler_params=params,
        cost_estimate=pl.CostEstimate(
            flops=2 * share * len(first),
            transcendentals=blocks * rows * seq * len(first) // (2 * nx),
            bytes_accessed=2 * q.size + 4 * seq * dh + 4 * q.size,
        ),
    )(x_index, q, *[ks[d] for d in first], *[vs[d] for d in first])
    return pl.pallas_call(
        lambda *refs: attend_last_kernel(*refs, offset=last, nx=nx),
        out_shape=jax.ShapeDtypeStruct(q.shape, jnp.bfloat16),
        in_specs=[smem] + [vmem] * 6,
        out_specs=vmem,
        compiler_params=params,
        cost_estimate=pl.CostEstimate(
            flops=2 * share,
            transcendentals=blocks * rows * seq // (2 * nx),
            bytes_accessed=2 * q.size + seq * dh + 8 * q.size,
        ),
    )(x_index, q, ks[last], vs[last], m, l, acc)


def gather_x(piece, nx, split_axis=0):
    if nx == 4:
        half = piece.shape[split_axis] // 2
        from_left = shifted(piece, "cx", 1)
        from_right = shifted(piece, "cx", -1)
        relay_a = shifted(lax.slice_in_dim(from_right, 0, half, axis=split_axis), "cx", -1)
        relay_b = shifted(
            lax.slice_in_dim(from_left, half, piece.shape[split_axis], axis=split_axis), "cx", 1
        )
        relay = jnp.concatenate([relay_a, relay_b], axis=split_axis)
        return [piece, from_right, relay, from_left]
    return [piece] + [shifted(piece, "cx", -d) for d in range(1, nx)]


def shards(inner_gate, outer_gate, signal, filters, bypass, query_rows, key_rows):
    local_rows, channels = signal.shape
    nz = lax.axis_size("cz")
    nx = lax.axis_size("cx")
    members = nz * nx
    heads = channels // DH
    my_x = lax.axis_index("cx")

    product = (inner_gate.astype(jnp.float32) * signal.astype(jnp.float32)).astype(jnp.bfloat16)
    previous = lax.ppermute(
        product,
        ("cz", "cx"),
        [(i, i + 1) for i in range(members - 1)],
    )
    hyena_out, qkv = hyena_local(previous, product, filters, outer_gate, bypass, query_rows, key_rows)

    spread = lax.all_to_all(qkv, "cz", 0, 0, tiled=True)
    q_here = spread[:, 0]
    got = gather_x(spread[:, 1:].transpose(1, 0, 2, 3), nx, 1)
    ks = [g[0] for g in got]
    vs = [g[1] for g in got]
    x_index = jnp.reshape(my_x, (1,)).astype(jnp.int32)
    out_here = attend_local(x_index, q_here, ks, vs, nx)
    returned = lax.all_to_all(out_here, "cz", 0, 0, tiled=True)
    attended = returned.transpose(1, 0, 2).reshape(local_rows, channels)
    return (hyena_out, attended)


def ctx_split(mesh):
    devices = np.asarray(mesh.devices)
    row = devices[0]
    try:
        nx = len({d.coords[0] for d in row})
    except Exception:
        nx = 4
    if row.size % nx:
        nx = 1
    return Mesh(devices.reshape(devices.shape[0], row.size // nx, nx), ("dp", "cz", "cx"))


def solution(mesh):
    split = ctx_split(mesh)
    rows = P(("dp", "cz", "cx"), None)
    placed = (rows, rows, rows, P(), P(), rows, rows)
    return jax.shard_map(
        shards,
        mesh=split,
        in_specs=placed,
        out_specs=(rows, rows),
        check_vma=False,
    )
```

```python
import math

import numpy as np
import jax
import jax.numpy as jnp
from jax import lax
from jax.sharding import Mesh, PartitionSpec as P
from jax.experimental import pallas as pl
from jax.experimental.pallas import tpu as pltpu

DH = 128
TAPS = 128


def shifted(array, axis, by):
    n = lax.axis_size(axis)
    return lax.ppermute(array, axis, [(i, (i + by) % n) for i in range(n)])


def band_dots(x, q_ref, k, mask, lane_group, rows, groups_per_chunk):
    bands = []
    for gg in range(groups_per_chunk):
        g = k * groups_per_chunk + gg
        row = q_ref[pl.ds(g, 1), :]
        rolled = pltpu.roll(jnp.broadcast_to(row, (rows, rows)), 0, 1, stride=1, stride_axis=0)
        bands.append(jnp.where(mask, rolled, 0.0))
    band = jnp.concatenate(bands, axis=0)
    hi = band.astype(jnp.bfloat16)
    lo = (band - hi.astype(jnp.float32)).astype(jnp.bfloat16)
    y = jnp.dot(hi, x, preferred_element_type=jnp.float32) + jnp.dot(
        lo, x, preferred_element_type=jnp.float32
    )
    acc = y[:rows]
    for gg in range(1, groups_per_chunk):
        acc = jnp.where(lane_group == gg, y[gg * rows : (gg + 1) * rows], acc)
    return acc


def conv_own_kernel(cur_ref, q_ref, part_ref, *, group_width):
    rows = cur_ref.shape[0]
    groups_per_chunk = 128 // group_width
    lane_group = lax.broadcasted_iota(jnp.int32, (rows, 128), 1) // group_width
    t = lax.broadcasted_iota(jnp.int32, (rows, rows), 0)
    r = lax.broadcasted_iota(jnp.int32, (rows, rows), 1)
    k = pl.program_id(0)
    part_ref[...] = band_dots(
        cur_ref[...], q_ref, k, r <= t, lane_group, rows, groups_per_chunk
    )


def conv_rim_kernel(prev_ref, cur_ref, q_ref, part_ref, outer_ref, bypass_ref, query_ref, key_ref, out_ref, heads_ref, *, group_width):
    rows = cur_ref.shape[0]
    groups_per_chunk = 128 // group_width
    lane_group = lax.broadcasted_iota(jnp.int32, (rows, 128), 1) // group_width
    t = lax.broadcasted_iota(jnp.int32, (rows, rows), 0)
    r = lax.broadcasted_iota(jnp.int32, (rows, rows), 1)
    k = pl.program_id(0)
    acc = band_dots(prev_ref[...], q_ref, k, r > t, lane_group, rows, groups_per_chunk)
    acc = acc + part_ref[...]
    product = cur_ref[...].astype(jnp.float32)
    outer = outer_ref[...].astype(jnp.float32)
    result = (outer * (acc + bypass_ref[...] * product)).astype(out_ref.dtype)
    out_ref[...] = result
    heads_ref[0, 0] = query_ref[...]
    heads_ref[0, 1] = key_ref[...]
    heads_ref[0, 2] = result


def hyena_local(prev, cur, filters, outer, bypass, query_rows, key_rows):
    rows, channels = outer.shape
    group_count, taps = filters.shape
    rotated = jnp.roll(filters[:, ::-1], 1, axis=1)
    width = channels // group_count
    chunks = channels // 128
    lanes = pl.BlockSpec((rows, 128), lambda k: (0, k))
    table = pl.BlockSpec((group_count, taps), lambda k: (0, 0))
    flops = 2 * 2 * 8 * rows * rows * channels
    part = pl.pallas_call(
        lambda *refs: conv_own_kernel(*refs, group_width=width),
        out_shape=jax.ShapeDtypeStruct((rows, channels), jnp.float32),
        grid=(chunks,),
        in_specs=[lanes, table],
        out_specs=lanes,
        cost_estimate=pl.CostEstimate(
            flops=flops, transcendentals=0, bytes_accessed=2 * cur.size + 4 * cur.size
        ),
    )(cur, rotated)
    return pl.pallas_call(
        lambda *refs: conv_rim_kernel(*refs, group_width=width),
        out_shape=(
            jax.ShapeDtypeStruct((rows, channels), jnp.bfloat16),
            jax.ShapeDtypeStruct((chunks, 3, rows, 128), jnp.bfloat16),
        ),
        grid=(chunks,),
        in_specs=[
            lanes, lanes, table, lanes, lanes,
            pl.BlockSpec((1, 128), lambda k: (0, k)),
            lanes, lanes,
        ],
        out_specs=(lanes, pl.BlockSpec((1, 3, rows, 128), lambda k: (k, 0, 0, 0))),
        cost_estimate=pl.CostEstimate(
            flops=flops, transcendentals=0, bytes_accessed=16 * cur.size
        ),
    )(prev, cur, rotated, part, outer, bypass.reshape(1, channels), query_rows, key_rows)


def piece_scores(q, k_ref, i, xd, x, rows, row_id, col_id, inv_root):
    length = (i + 1) * rows
    dh = k_ref.shape[-1]
    k = k_ref[: i + 1].reshape(length, dh)
    s = lax.dot_general(
        q, k, (((1,), (1,)), ((), ())), preferred_element_type=jnp.float32
    ) * inv_root
    visible = (xd * rows + col_id) <= (x * rows + row_id)
    tail = jnp.where(visible, s[:, length - rows :], -1e30)
    head = s[:, : length - rows] if i > 0 else None
    return head, tail, visible


def piece_max(head, tail):
    m = jnp.max(tail, axis=1, keepdims=True)
    if head is not None:
        m = jnp.maximum(m, jnp.max(head, axis=1, keepdims=True))
    return m


def piece_sums(head, tail, visible, v_ref, i, highest, rows):
    dh = v_ref.shape[-1]
    w_tail = jnp.where(visible, jnp.exp(tail - highest), 0.0)
    part_sum = jnp.sum(w_tail, axis=1, keepdims=True)
    part = jnp.dot(w_tail.astype(jnp.bfloat16), v_ref[i], preferred_element_type=jnp.float32)
    if head is not None:
        w_head = jnp.exp(head - highest)
        part_sum = part_sum + jnp.sum(w_head, axis=1, keepdims=True)
        v_head = v_ref[:i].reshape(i * rows, dh)
        part = part + jnp.dot(
            w_head.astype(jnp.bfloat16), v_head, preferred_element_type=jnp.float32
        )
    return part_sum, part


def attend_first_kernel(x_ref, q_ref, *refs, offsets, nx):
    n = len(offsets)
    k_refs = refs[:n]
    v_refs = refs[n : 2 * n]
    m_ref, l_ref, acc_ref = refs[2 * n :]
    x = x_ref[0]
    blocks, rows, dh = q_ref.shape
    inv_root = 1.0 / math.sqrt(DH)
    row_id = lax.broadcasted_iota(jnp.int32, (rows, rows), 0)
    col_id = lax.broadcasted_iota(jnp.int32, (rows, rows), 1)
    for i in range(blocks):
        q = q_ref[i]
        pieces = []
        for j, d in enumerate(offsets):
            xd = lax.rem(x + d, nx)
            pieces.append(piece_scores(q, k_refs[j], i, xd, x, rows, row_id, col_id, inv_root))
        highest = None
        for head, tail, _ in pieces:
            m = piece_max(head, tail)
            highest = m if highest is None else jnp.maximum(highest, m)
        total = None
        acc = None
        for j, (head, tail, visible) in enumerate(pieces):
            part_sum, part = piece_sums(head, tail, visible, v_refs[j], i, highest, rows)
            total = part_sum if total is None else total + part_sum
            acc = part if acc is None else acc + part
        m_ref[i] = highest
        l_ref[i] = total
        acc_ref[i] = acc


def attend_last_kernel(x_ref, q_ref, k_ref, v_ref, m_ref, l_ref, acc_ref, o_ref, *, offset, nx):
    x = x_ref[0]
    blocks, rows, dh = q_ref.shape
    inv_root = 1.0 / math.sqrt(DH)
    row_id = lax.broadcasted_iota(jnp.int32, (rows, rows), 0)
    col_id = lax.broadcasted_iota(jnp.int32, (rows, rows), 1)
    xd = lax.rem(x + offset, nx)
    for i in range(blocks):
        head, tail, visible = piece_scores(q_ref[i], k_ref, i, xd, x, rows, row_id, col_id, inv_root)
        earlier = m_ref[i]
        highest = jnp.maximum(earlier, piece_max(head, tail))
        scale = jnp.exp(earlier - highest)
        part_sum, part = piece_sums(head, tail, visible, v_ref, i, highest, rows)
        total = l_ref[i] * scale + part_sum
        acc = acc_ref[i] * scale + part
        o_ref[i] = (acc / total).astype(o_ref.dtype)


def attend_local(x_index, q, ks, vs, nx):
    blocks, rows, dh = q.shape
    seq = nx * blocks * rows
    vmem = pl.BlockSpec(memory_space=pltpu.VMEM)
    smem = pl.BlockSpec(memory_space=pltpu.SMEM)
    params = pltpu.CompilerParams(vmem_limit_bytes=48 * 1024 * 1024)
    last = 2 if nx == 4 else nx - 1
    first = [d for d in range(nx) if d != last]
    share = blocks * rows * seq * dh // nx
    m, l, acc = pl.pallas_call(
        lambda *refs: attend_first_kernel(*refs, offsets=first, nx=nx),
        out_shape=(
            jax.ShapeDtypeStruct((blocks, rows, 1), jnp.float32),
            jax.ShapeDtypeStruct((blocks, rows, 1), jnp.float32),
            jax.ShapeDtypeStruct((blocks, rows, dh), jnp.float32),
        ),
        in_specs=[smem] + [vmem] * (1 + 2 * len(first)),
        out_specs=(vmem, vmem, vmem),
        compiler_params=params,
        cost_estimate=pl.CostEstimate(
            flops=2 * share * len(first),
            transcendentals=blocks * rows * seq * len(first) // (2 * nx),
            bytes_accessed=2 * q.size + 4 * seq * dh + 4 * q.size,
        ),
    )(x_index, q, *[ks[d] for d in first], *[vs[d] for d in first])
    return pl.pallas_call(
        lambda *refs: attend_last_kernel(*refs, offset=last, nx=nx),
        out_shape=jax.ShapeDtypeStruct(q.shape, jnp.bfloat16),
        in_specs=[smem] + [vmem] * 6,
        out_specs=vmem,
        compiler_params=params,
        cost_estimate=pl.CostEstimate(
            flops=2 * share,
            transcendentals=blocks * rows * seq // (2 * nx),
            bytes_accessed=2 * q.size + seq * dh + 8 * q.size,
        ),
    )(x_index, q, ks[last], vs[last], m, l, acc)


def gather_x(piece, nx, split_axis=0):
    if nx == 4:
        half = piece.shape[split_axis] // 2
        from_left = shifted(piece, "cx", 1)
        from_right = shifted(piece, "cx", -1)
        relay_a = shifted(lax.slice_in_dim(from_right, 0, half, axis=split_axis), "cx", -1)
        relay_b = shifted(
            lax.slice_in_dim(from_left, half, piece.shape[split_axis], axis=split_axis), "cx", 1
        )
        relay = jnp.concatenate([relay_a, relay_b], axis=split_axis)
        return [piece, from_right, relay, from_left]
    return [piece] + [shifted(piece, "cx", -d) for d in range(1, nx)]


def shards(inner_gate, outer_gate, signal, filters, bypass, query_rows, key_rows):
    local_rows, channels = signal.shape
    nz = lax.axis_size("cz")
    nx = lax.axis_size("cx")
    members = nz * nx
    heads = channels // DH
    my_x = lax.axis_index("cx")

    product = (inner_gate.astype(jnp.float32) * signal.astype(jnp.float32)).astype(jnp.bfloat16)
    previous = lax.ppermute(
        product,
        ("cz", "cx"),
        [(i, i + 1) for i in range(members - 1)],
    )
    hyena_out, qkv = hyena_local(previous, product, filters, outer_gate, bypass, query_rows, key_rows)

    spread = lax.all_to_all(qkv, "cz", 0, 0, tiled=True)
    q_here = spread[:, 0]
    got = gather_x(spread[:, 1:].transpose(1, 0, 2, 3), nx, 1)
    ks = [g[0] for g in got]
    vs = [g[1] for g in got]
    x_index = jnp.reshape(my_x, (1,)).astype(jnp.int32)
    out_here = attend_local(x_index, q_here, ks, vs, nx)
    returned = lax.all_to_all(out_here, "cz", 0, 0, tiled=True)
    attended = returned.transpose(1, 0, 2).reshape(local_rows, channels)
    return (hyena_out, attended)


def ctx_split(mesh):
    devices = np.asarray(mesh.devices)
    row = devices[0]
    try:
        nx = len({d.coords[0] for d in row})
    except Exception:
        nx = 4
    if row.size % nx:
        nx = 1
    return Mesh(devices.reshape(devices.shape[0], row.size // nx, nx), ("dp", "cz", "cx"))


def solution(mesh):
    split = ctx_split(mesh)
    rows = P(("dp", "cz", "cx"), None)
    placed = (rows, rows, rows, P(), P(), rows, rows)
    return jax.shard_map(
        shards,
        mesh=split,
        in_specs=placed,
        out_specs=(rows, rows),
        check_vma=False,
    )
```

```python
import math

import numpy as np
import jax
import jax.numpy as jnp
from jax import lax
from jax.sharding import Mesh, PartitionSpec as P
from jax.experimental import pallas as pl
from jax.experimental.pallas import tpu as pltpu

DH = 128
TAPS = 128


def shifted(array, axis, by):
    n = lax.axis_size(axis)
    return lax.ppermute(array, axis, [(i, (i + by) % n) for i in range(n)])


def band_dots(x, q_ref, k, mask, lane_group, rows, groups_per_chunk):
    bands = []
    for gg in range(groups_per_chunk):
        g = k * groups_per_chunk + gg
        row = q_ref[pl.ds(g, 1), :]
        rolled = pltpu.roll(jnp.broadcast_to(row, (rows, rows)), 0, 1, stride=1, stride_axis=0)
        bands.append(jnp.where(mask, rolled, 0.0))
    band = jnp.concatenate(bands, axis=0)
    hi = band.astype(jnp.bfloat16)
    lo = (band - hi.astype(jnp.float32)).astype(jnp.bfloat16)
    y = jnp.dot(hi, x, preferred_element_type=jnp.float32) + jnp.dot(
        lo, x, preferred_element_type=jnp.float32
    )
    acc = y[:rows]
    for gg in range(1, groups_per_chunk):
        acc = jnp.where(lane_group == gg, y[gg * rows : (gg + 1) * rows], acc)
    return acc


def conv_own_kernel(cur_ref, q_ref, part_ref, *, group_width):
    rows, channels = cur_ref.shape
    groups_per_chunk = 128 // group_width
    lane_group = lax.broadcasted_iota(jnp.int32, (rows, 128), 1) // group_width
    t = lax.broadcasted_iota(jnp.int32, (rows, rows), 0)
    r = lax.broadcasted_iota(jnp.int32, (rows, rows), 1)
    lower = r <= t

    def chunk(k, carry):
        col = pl.multiple_of(k * 128, 128)
        x = cur_ref[:, pl.ds(col, 128)]
        part_ref[:, pl.ds(col, 128)] = band_dots(
            x, q_ref, k, lower, lane_group, rows, groups_per_chunk
        )
        return carry

    lax.fori_loop(0, channels // 128, chunk, 0)


def conv_rim_kernel(prev_ref, cur_ref, q_ref, part_ref, outer_ref, bypass_ref, query_ref, key_ref, out_ref, heads_ref, *, group_width):
    rows, channels = cur_ref.shape
    groups_per_chunk = 128 // group_width
    lane_group = lax.broadcasted_iota(jnp.int32, (rows, 128), 1) // group_width
    t = lax.broadcasted_iota(jnp.int32, (rows, rows), 0)
    r = lax.broadcasted_iota(jnp.int32, (rows, rows), 1)
    upper = r > t

    def chunk(k, carry):
        col = pl.multiple_of(k * 128, 128)
        x = prev_ref[:, pl.ds(col, 128)]
        acc = band_dots(x, q_ref, k, upper, lane_group, rows, groups_per_chunk)
        acc = acc + part_ref[:, pl.ds(col, 128)]
        product = cur_ref[:, pl.ds(col, 128)].astype(jnp.float32)
        outer = outer_ref[:, pl.ds(col, 128)].astype(jnp.float32)
        bypass = bypass_ref[:, pl.ds(col, 128)]
        result = (outer * (acc + bypass * product)).astype(out_ref.dtype)
        out_ref[:, pl.ds(col, 128)] = result
        heads_ref[k, 0] = query_ref[:, pl.ds(col, 128)]
        heads_ref[k, 1] = key_ref[:, pl.ds(col, 128)]
        heads_ref[k, 2] = result
        return carry

    lax.fori_loop(0, channels // 128, chunk, 0)


def hyena_local(prev, cur, filters, outer, bypass, query_rows, key_rows):
    rows, channels = outer.shape
    group_count, taps = filters.shape
    rotated = jnp.roll(filters[:, ::-1], 1, axis=1)
    width = channels // group_count
    vmem = pl.BlockSpec(memory_space=pltpu.VMEM)
    flops = 2 * 2 * 8 * rows * rows * channels
    part = pl.pallas_call(
        lambda *refs: conv_own_kernel(*refs, group_width=width),
        out_shape=jax.ShapeDtypeStruct((rows, channels), jnp.float32),
        in_specs=[vmem] * 2,
        out_specs=vmem,
        cost_estimate=pl.CostEstimate(
            flops=flops, transcendentals=0, bytes_accessed=2 * cur.size + 4 * cur.size
        ),
    )(cur, rotated)
    return pl.pallas_call(
        lambda *refs: conv_rim_kernel(*refs, group_width=width),
        out_shape=(
            jax.ShapeDtypeStruct((rows, channels), jnp.bfloat16),
            jax.ShapeDtypeStruct((channels // DH, 3, rows, DH), jnp.bfloat16),
        ),
        in_specs=[vmem] * 8,
        out_specs=(vmem, vmem),
        cost_estimate=pl.CostEstimate(
            flops=flops, transcendentals=0, bytes_accessed=16 * cur.size
        ),
    )(prev, cur, rotated, part, outer, bypass.reshape(1, channels), query_rows, key_rows)


def piece_scores(q, k_ref, i, xd, x, rows, row_id, col_id, inv_root):
    length = (i + 1) * rows
    dh = k_ref.shape[-1]
    k = k_ref[: i + 1].reshape(length, dh)
    s = lax.dot_general(
        q, k, (((1,), (1,)), ((), ())), preferred_element_type=jnp.float32
    ) * inv_root
    visible = (xd * rows + col_id) <= (x * rows + row_id)
    tail = jnp.where(visible, s[:, length - rows :], -1e30)
    head = s[:, : length - rows] if i > 0 else None
    return head, tail, visible


def piece_max(head, tail):
    m = jnp.max(tail, axis=1, keepdims=True)
    if head is not None:
        m = jnp.maximum(m, jnp.max(head, axis=1, keepdims=True))
    return m


def piece_sums(head, tail, visible, v_ref, i, highest, rows):
    dh = v_ref.shape[-1]
    w_tail = jnp.where(visible, jnp.exp(tail - highest), 0.0)
    part_sum = jnp.sum(w_tail, axis=1, keepdims=True)
    part = jnp.dot(w_tail.astype(jnp.bfloat16), v_ref[i], preferred_element_type=jnp.float32)
    if head is not None:
        w_head = jnp.exp(head - highest)
        part_sum = part_sum + jnp.sum(w_head, axis=1, keepdims=True)
        v_head = v_ref[:i].reshape(i * rows, dh)
        part = part + jnp.dot(
            w_head.astype(jnp.bfloat16), v_head, preferred_element_type=jnp.float32
        )
    return part_sum, part


def attend_merge_kernel(x_ref, q_ref, *refs, offsets, nx, prior, final):
    n = len(offsets)
    k_refs = refs[:n]
    v_refs = refs[n : 2 * n]
    rest = refs[2 * n :]
    if prior:
        m_in, l_in, acc_in = rest[:3]
        rest = rest[3:]
    x = x_ref[0]
    blocks, rows, dh = q_ref.shape
    inv_root = 1.0 / math.sqrt(DH)
    row_id = lax.broadcasted_iota(jnp.int32, (rows, rows), 0)
    col_id = lax.broadcasted_iota(jnp.int32, (rows, rows), 1)
    for i in range(blocks):
        q = q_ref[i]
        pieces = []
        for j, d in enumerate(offsets):
            xd = lax.rem(x + d, nx)
            pieces.append(piece_scores(q, k_refs[j], i, xd, x, rows, row_id, col_id, inv_root))
        highest = m_in[i] if prior else None
        for head, tail, _ in pieces:
            m = piece_max(head, tail)
            highest = m if highest is None else jnp.maximum(highest, m)
        if prior:
            scale = jnp.exp(m_in[i] - highest)
            total = l_in[i] * scale
            acc = acc_in[i] * scale
        else:
            total = None
            acc = None
        for j, (head, tail, visible) in enumerate(pieces):
            part_sum, part = piece_sums(head, tail, visible, v_refs[j], i, highest, rows)
            total = part_sum if total is None else total + part_sum
            acc = part if acc is None else acc + part
        if final:
            rest[0][i] = (acc / total).astype(rest[0].dtype)
        else:
            m_out, l_out, acc_out = rest
            m_out[i] = highest
            l_out[i] = total
            acc_out[i] = acc


def attend_local(x_index, q, ks, vs, nx):
    blocks, rows, dh = q.shape
    seq = nx * blocks * rows
    vmem = pl.BlockSpec(memory_space=pltpu.VMEM)
    smem = pl.BlockSpec(memory_space=pltpu.SMEM)
    params = pltpu.CompilerParams(vmem_limit_bytes=48 * 1024 * 1024)
    if nx == 4:
        stages = [[0], [1, 3], [2]]
    else:
        stages = [list(range(nx))]
    share = blocks * rows * seq * dh // nx
    state = ()
    state_shapes = (
        jax.ShapeDtypeStruct((blocks, rows, 1), jnp.float32),
        jax.ShapeDtypeStruct((blocks, rows, 1), jnp.float32),
        jax.ShapeDtypeStruct((blocks, rows, dh), jnp.float32),
    )
    for n_stage, offsets in enumerate(stages):
        prior = n_stage > 0
        final = n_stage == len(stages) - 1
        out_shape = jax.ShapeDtypeStruct(q.shape, jnp.bfloat16) if final else state_shapes
        out_specs = vmem if final else (vmem, vmem, vmem)
        result = pl.pallas_call(
            lambda *refs, offsets=offsets, prior=prior, final=final: attend_merge_kernel(
                *refs, offsets=offsets, nx=nx, prior=prior, final=final
            ),
            out_shape=out_shape,
            in_specs=[smem] + [vmem] * (1 + 2 * len(offsets) + (3 if prior else 0)),
            out_specs=out_specs,
            compiler_params=params,
            cost_estimate=pl.CostEstimate(
                flops=2 * share * len(offsets),
                transcendentals=blocks * rows * seq * len(offsets) // (2 * nx),
                bytes_accessed=2 * q.size + seq * dh * len(offsets) // nx + 8 * q.size,
            ),
        )(x_index, q, *[ks[d] for d in offsets], *[vs[d] for d in offsets], *state)
        state = result if not final else ()
    return result


def gather_x(piece, nx, split_axis=0):
    if nx == 4:
        half = piece.shape[split_axis] // 2
        from_left = shifted(piece, "cx", 1)
        from_right = shifted(piece, "cx", -1)
        relay_a = shifted(lax.slice_in_dim(from_right, 0, half, axis=split_axis), "cx", -1)
        relay_b = shifted(
            lax.slice_in_dim(from_left, half, piece.shape[split_axis], axis=split_axis), "cx", 1
        )
        relay = jnp.concatenate([relay_a, relay_b], axis=split_axis)
        return [piece, from_right, relay, from_left]
    return [piece] + [shifted(piece, "cx", -d) for d in range(1, nx)]


def shards(inner_gate, outer_gate, signal, filters, bypass, query_rows, key_rows):
    local_rows, channels = signal.shape
    nz = lax.axis_size("cz")
    nx = lax.axis_size("cx")
    members = nz * nx
    heads = channels // DH
    my_x = lax.axis_index("cx")

    product = (inner_gate.astype(jnp.float32) * signal.astype(jnp.float32)).astype(jnp.bfloat16)
    previous = lax.ppermute(
        product,
        ("cz", "cx"),
        [(i, i + 1) for i in range(members - 1)],
    )
    hyena_out, qkv = hyena_local(previous, product, filters, outer_gate, bypass, query_rows, key_rows)

    spread = lax.all_to_all(qkv, "cz", 0, 0, tiled=True)
    q_here = spread[:, 0]
    got = gather_x(spread[:, 1:].transpose(1, 0, 2, 3), nx, 1)
    ks = [g[0] for g in got]
    vs = [g[1] for g in got]
    x_index = jnp.reshape(my_x, (1,)).astype(jnp.int32)
    out_here = attend_local(x_index, q_here, ks, vs, nx)
    returned = lax.all_to_all(out_here, "cz", 0, 0, tiled=True)
    attended = returned.transpose(1, 0, 2).reshape(local_rows, channels)
    return (hyena_out, attended)


def ctx_split(mesh):
    devices = np.asarray(mesh.devices)
    row = devices[0]
    try:
        nx = len({d.coords[0] for d in row})
    except Exception:
        nx = 4
    if row.size % nx:
        nx = 1
    return Mesh(devices.reshape(devices.shape[0], row.size // nx, nx), ("dp", "cz", "cx"))


def solution(mesh):
    split = ctx_split(mesh)
    rows = P(("dp", "cz", "cx"), None)
    placed = (rows, rows, rows, P(), P(), rows, rows)
    return jax.shard_map(
        shards,
        mesh=split,
        in_specs=placed,
        out_specs=(rows, rows),
        check_vma=False,
    )
```

```python
import math

import numpy as np
import jax
import jax.numpy as jnp
from jax import lax
from jax.sharding import Mesh, PartitionSpec as P
from jax.experimental import pallas as pl
from jax.experimental.pallas import tpu as pltpu

DH = 128
TAPS = 128


def shifted(array, axis, by):
    n = lax.axis_size(axis)
    return lax.ppermute(array, axis, [(i, (i + by) % n) for i in range(n)])


def band_dots(x, q_ref, k, mask, lane_group, rows, groups_per_chunk):
    bands = []
    for gg in range(groups_per_chunk):
        g = k * groups_per_chunk + gg
        row = q_ref[pl.ds(g, 1), :]
        rolled = pltpu.roll(jnp.broadcast_to(row, (rows, rows)), 0, 1, stride=1, stride_axis=0)
        bands.append(jnp.where(mask, rolled, 0.0))
    band = jnp.concatenate(bands, axis=0)
    hi = band.astype(jnp.bfloat16)
    lo = (band - hi.astype(jnp.float32)).astype(jnp.bfloat16)
    y = jnp.dot(hi, x, preferred_element_type=jnp.float32) + jnp.dot(
        lo, x, preferred_element_type=jnp.float32
    )
    acc = y[:rows]
    for gg in range(1, groups_per_chunk):
        acc = jnp.where(lane_group == gg, y[gg * rows : (gg + 1) * rows], acc)
    return acc


def conv_own_kernel(cur_ref, q_ref, part_ref, *, group_width):
    rows, channels = cur_ref.shape
    groups_per_chunk = 128 // group_width
    lane_group = lax.broadcasted_iota(jnp.int32, (rows, 128), 1) // group_width
    t = lax.broadcasted_iota(jnp.int32, (rows, rows), 0)
    r = lax.broadcasted_iota(jnp.int32, (rows, rows), 1)
    lower = r <= t

    def chunk(k, carry):
        col = pl.multiple_of(k * 128, 128)
        x = cur_ref[:, pl.ds(col, 128)]
        part_ref[:, pl.ds(col, 128)] = band_dots(
            x, q_ref, k, lower, lane_group, rows, groups_per_chunk
        )
        return carry

    lax.fori_loop(0, channels // 128, chunk, 0)


def conv_rim_kernel(prev_ref, cur_ref, q_ref, part_ref, outer_ref, bypass_ref, query_ref, key_ref, out_ref, heads_ref, *, group_width):
    rows, channels = cur_ref.shape
    groups_per_chunk = 128 // group_width
    lane_group = lax.broadcasted_iota(jnp.int32, (rows, 128), 1) // group_width
    t = lax.broadcasted_iota(jnp.int32, (rows, rows), 0)
    r = lax.broadcasted_iota(jnp.int32, (rows, rows), 1)
    upper = r > t

    def chunk(k, carry):
        col = pl.multiple_of(k * 128, 128)
        x = prev_ref[:, pl.ds(col, 128)]
        acc = band_dots(x, q_ref, k, upper, lane_group, rows, groups_per_chunk)
        acc = acc + part_ref[:, pl.ds(col, 128)]
        product = cur_ref[:, pl.ds(col, 128)].astype(jnp.float32)
        outer = outer_ref[:, pl.ds(col, 128)].astype(jnp.float32)
        bypass = bypass_ref[:, pl.ds(col, 128)]
        result = (outer * (acc + bypass * product)).astype(out_ref.dtype)
        out_ref[:, pl.ds(col, 128)] = result
        heads_ref[k, 0] = query_ref[:, pl.ds(col, 128)]
        heads_ref[k, 1] = key_ref[:, pl.ds(col, 128)]
        heads_ref[k, 2] = result
        return carry

    lax.fori_loop(0, channels // 128, chunk, 0)


def hyena_local(prev, cur, filters, outer, bypass, query_rows, key_rows):
    rows, channels = outer.shape
    group_count, taps = filters.shape
    rotated = jnp.roll(filters[:, ::-1], 1, axis=1)
    width = channels // group_count
    vmem = pl.BlockSpec(memory_space=pltpu.VMEM)
    flops = 2 * 2 * 8 * rows * rows * channels
    part = pl.pallas_call(
        lambda *refs: conv_own_kernel(*refs, group_width=width),
        out_shape=jax.ShapeDtypeStruct((rows, channels), jnp.float32),
        in_specs=[vmem] * 2,
        out_specs=vmem,
        cost_estimate=pl.CostEstimate(
            flops=flops, transcendentals=0, bytes_accessed=2 * cur.size + 4 * cur.size
        ),
    )(cur, rotated)
    return pl.pallas_call(
        lambda *refs: conv_rim_kernel(*refs, group_width=width),
        out_shape=(
            jax.ShapeDtypeStruct((rows, channels), jnp.bfloat16),
            jax.ShapeDtypeStruct((channels // DH, 3, rows, DH), jnp.bfloat16),
        ),
        in_specs=[vmem] * 8,
        out_specs=(vmem, vmem),
        cost_estimate=pl.CostEstimate(
            flops=flops, transcendentals=0, bytes_accessed=16 * cur.size
        ),
    )(prev, cur, rotated, part, outer, bypass.reshape(1, channels), query_rows, key_rows)


def piece_scores(q, k_ref, i, xd, x, rows, row_id, col_id, inv_root):
    length = (i + 1) * rows
    dh = k_ref.shape[-1]
    k = k_ref[: i + 1].reshape(length, dh)
    s = lax.dot_general(
        q, k, (((1,), (1,)), ((), ())), preferred_element_type=jnp.float32
    ) * inv_root
    visible = (xd * rows + col_id) <= (x * rows + row_id)
    tail = jnp.where(visible, s[:, length - rows :], -1e30)
    head = s[:, : length - rows] if i > 0 else None
    return head, tail, visible


def piece_max(head, tail):
    m = jnp.max(tail, axis=1, keepdims=True)
    if head is not None:
        m = jnp.maximum(m, jnp.max(head, axis=1, keepdims=True))
    return m


def piece_sums(head, tail, visible, v_ref, i, highest, rows):
    dh = v_ref.shape[-1]
    w_tail = jnp.where(visible, jnp.exp(tail - highest), 0.0)
    part_sum = jnp.sum(w_tail, axis=1, keepdims=True)
    part = jnp.dot(w_tail.astype(jnp.bfloat16), v_ref[i], preferred_element_type=jnp.float32)
    if head is not None:
        w_head = jnp.exp(head - highest)
        part_sum = part_sum + jnp.sum(w_head, axis=1, keepdims=True)
        v_head = v_ref[:i].reshape(i * rows, dh)
        part = part + jnp.dot(
            w_head.astype(jnp.bfloat16), v_head, preferred_element_type=jnp.float32
        )
    return part_sum, part


def attend_first_kernel(x_ref, q_ref, *refs, offsets, nx):
    n = len(offsets)
    k_refs = refs[:n]
    v_refs = refs[n : 2 * n]
    stats_ref, acc_ref = refs[2 * n :]
    x = x_ref[0]
    blocks, rows, dh = q_ref.shape
    inv_root = 1.0 / math.sqrt(DH)
    row_id = lax.broadcasted_iota(jnp.int32, (rows, rows), 0)
    col_id = lax.broadcasted_iota(jnp.int32, (rows, rows), 1)
    stats = jnp.zeros(stats_ref.shape, jnp.float32)
    for i in range(blocks):
        q = q_ref[i]
        pieces = []
        for j, d in enumerate(offsets):
            xd = lax.rem(x + d, nx)
            pieces.append(piece_scores(q, k_refs[j], i, xd, x, rows, row_id, col_id, inv_root))
        highest = None
        for head, tail, _ in pieces:
            m = piece_max(head, tail)
            highest = m if highest is None else jnp.maximum(highest, m)
        total = None
        acc = None
        for j, (head, tail, visible) in enumerate(pieces):
            part_sum, part = piece_sums(head, tail, visible, v_refs[j], i, highest, rows)
            total = part_sum if total is None else total + part_sum
            acc = part if acc is None else acc + part
        stats = jnp.where(col_id == 2 * i, highest, jnp.where(col_id == 2 * i + 1, total, stats))
        acc_ref[i] = acc
    stats_ref[...] = stats


def attend_last_kernel(x_ref, q_ref, k_ref, v_ref, stats_ref, acc_ref, o_ref, *, offset, nx):
    x = x_ref[0]
    blocks, rows, dh = q_ref.shape
    inv_root = 1.0 / math.sqrt(DH)
    row_id = lax.broadcasted_iota(jnp.int32, (rows, rows), 0)
    col_id = lax.broadcasted_iota(jnp.int32, (rows, rows), 1)
    xd = lax.rem(x + offset, nx)
    for i in range(blocks):
        head, tail, visible = piece_scores(q_ref[i], k_ref, i, xd, x, rows, row_id, col_id, inv_root)
        earlier = stats_ref[:, 2 * i : 2 * i + 1]
        highest = jnp.maximum(earlier, piece_max(head, tail))
        scale = jnp.exp(earlier - highest)
        part_sum, part = piece_sums(head, tail, visible, v_ref, i, highest, rows)
        total = stats_ref[:, 2 * i + 1 : 2 * i + 2] * scale + part_sum
        acc = acc_ref[i] * scale + part
        o_ref[i] = (acc / total).astype(o_ref.dtype)


def attend_local(x_index, q, ks, vs, nx):
    blocks, rows, dh = q.shape
    seq = nx * blocks * rows
    vmem = pl.BlockSpec(memory_space=pltpu.VMEM)
    smem = pl.BlockSpec(memory_space=pltpu.SMEM)
    params = pltpu.CompilerParams(vmem_limit_bytes=48 * 1024 * 1024)
    last = 2 if nx == 4 else nx - 1
    first = [d for d in range(nx) if d != last]
    share = blocks * rows * seq * dh // nx
    stats, acc = pl.pallas_call(
        lambda *refs: attend_first_kernel(*refs, offsets=first, nx=nx),
        out_shape=(
            jax.ShapeDtypeStruct((rows, 128), jnp.float32),
            jax.ShapeDtypeStruct((blocks, rows, dh), jnp.float32),
        ),
        in_specs=[smem] + [vmem] * (1 + 2 * len(first)),
        out_specs=(vmem, vmem),
        compiler_params=params,
        cost_estimate=pl.CostEstimate(
            flops=2 * share * len(first),
            transcendentals=blocks * rows * seq * len(first) // (2 * nx),
            bytes_accessed=2 * q.size + 4 * seq * dh + 4 * q.size,
        ),
    )(x_index, q, *[ks[d] for d in first], *[vs[d] for d in first])
    return pl.pallas_call(
        lambda *refs: attend_last_kernel(*refs, offset=last, nx=nx),
        out_shape=jax.ShapeDtypeStruct(q.shape, jnp.bfloat16),
        in_specs=[smem] + [vmem] * 5,
        out_specs=vmem,
        compiler_params=params,
        cost_estimate=pl.CostEstimate(
            flops=2 * share,
            transcendentals=blocks * rows * seq // (2 * nx),
            bytes_accessed=2 * q.size + seq * dh + 8 * q.size,
        ),
    )(x_index, q, ks[last], vs[last], stats, acc)


def gather_x(piece, nx, split_axis=0):
    if nx == 4:
        half = piece.shape[split_axis] // 2
        from_left = shifted(piece, "cx", 1)
        from_right = shifted(piece, "cx", -1)
        relay_a = shifted(lax.slice_in_dim(from_right, 0, half, axis=split_axis), "cx", -1)
        relay_b = shifted(
            lax.slice_in_dim(from_left, half, piece.shape[split_axis], axis=split_axis), "cx", 1
        )
        relay = jnp.concatenate([relay_a, relay_b], axis=split_axis)
        return [piece, from_right, relay, from_left]
    return [piece] + [shifted(piece, "cx", -d) for d in range(1, nx)]


def shards(inner_gate, outer_gate, signal, filters, bypass, query_rows, key_rows):
    local_rows, channels = signal.shape
    nz = lax.axis_size("cz")
    nx = lax.axis_size("cx")
    members = nz * nx
    heads = channels // DH
    my_x = lax.axis_index("cx")

    product = (inner_gate.astype(jnp.float32) * signal.astype(jnp.float32)).astype(jnp.bfloat16)
    previous = lax.ppermute(
        product,
        ("cz", "cx"),
        [(i, i + 1) for i in range(members - 1)],
    )
    hyena_out, qkv = hyena_local(previous, product, filters, outer_gate, bypass, query_rows, key_rows)

    spread = lax.all_to_all(qkv, "cz", 0, 0, tiled=True)
    q_here = spread[:, 0]
    got = gather_x(spread[:, 1:].transpose(1, 0, 2, 3), nx, 1)
    ks = [g[0] for g in got]
    vs = [g[1] for g in got]
    x_index = jnp.reshape(my_x, (1,)).astype(jnp.int32)
    out_here = attend_local(x_index, q_here, ks, vs, nx)
    returned = lax.all_to_all(out_here, "cz", 0, 0, tiled=True)
    attended = returned.transpose(1, 0, 2).reshape(local_rows, channels)
    return (hyena_out, attended)


def ctx_split(mesh):
    devices = np.asarray(mesh.devices)
    row = devices[0]
    try:
        nx = len({d.coords[0] for d in row})
    except Exception:
        nx = 4
    if row.size % nx:
        nx = 1
    return Mesh(devices.reshape(devices.shape[0], row.size // nx, nx), ("dp", "cz", "cx"))


def solution(mesh):
    split = ctx_split(mesh)
    rows = P(("dp", "cz", "cx"), None)
    placed = (rows, rows, rows, P(), P(), rows, rows)
    return jax.shard_map(
        shards,
        mesh=split,
        in_specs=placed,
        out_specs=(rows, rows),
        check_vma=False,
    )
```

```python
import math

import numpy as np
import jax
import jax.numpy as jnp
from jax import lax
from jax.sharding import Mesh, PartitionSpec as P
from jax.experimental import pallas as pl
from jax.experimental.pallas import tpu as pltpu

DH = 128
TAPS = 128


def shifted(array, axis, by):
    n = lax.axis_size(axis)
    return lax.ppermute(array, axis, [(i, (i + by) % n) for i in range(n)])


def conv_kernel(prev_ref, cur_ref, q_ref, outer_ref, bypass_ref, query_ref, key_ref, out_ref, heads_ref, *, group_width):
    rows, channels = cur_ref.shape
    window = q_ref.shape[1]
    groups_per_chunk = 128 // group_width
    lane_group = lax.broadcasted_iota(jnp.int32, (rows, 128), 1) // group_width

    def chunk(k, carry):
        col = pl.multiple_of(k * 128, 128)
        bands = []
        for gg in range(groups_per_chunk):
            g = k * groups_per_chunk + gg
            row = q_ref[pl.ds(g, 1), :]
            bands.append(
                pltpu.roll(jnp.broadcast_to(row, (rows, window)), 0, 1, stride=1, stride_axis=0)
            )
        band = jnp.concatenate(bands, axis=0)
        hi = band.astype(jnp.bfloat16)
        lo = (band - hi.astype(jnp.float32)).astype(jnp.bfloat16)
        x_prev = prev_ref[:, pl.ds(col, 128)]
        x_cur = cur_ref[:, pl.ds(col, 128)]
        y = None
        for half in (hi, lo):
            for part, x in ((half[:, :rows], x_prev), (half[:, rows:], x_cur)):
                d = jnp.dot(part, x, preferred_element_type=jnp.float32)
                y = d if y is None else y + d
        acc = y[:rows]
        for gg in range(1, groups_per_chunk):
            acc = jnp.where(lane_group == gg, y[gg * rows : (gg + 1) * rows], acc)
        product = x_cur.astype(jnp.float32)
        outer = outer_ref[:, pl.ds(col, 128)].astype(jnp.float32)
        bypass = bypass_ref[:, pl.ds(col, 128)]
        result = (outer * (acc + bypass * product)).astype(out_ref.dtype)
        out_ref[:, pl.ds(col, 128)] = result
        heads_ref[k, 0] = query_ref[:, pl.ds(col, 128)]
        heads_ref[k, 1] = key_ref[:, pl.ds(col, 128)]
        heads_ref[k, 2] = result
        return carry

    lax.fori_loop(0, channels // 128, chunk, 0)


def hyena_local(prev, cur, filters, outer, bypass, query_rows, key_rows):
    rows, channels = outer.shape
    group_count, taps = filters.shape
    padded = jnp.concatenate(
        [
            jnp.zeros((group_count, 1), jnp.float32),
            filters[:, ::-1],
            jnp.zeros((group_count, 2 * rows - taps - 1), jnp.float32),
        ],
        axis=1,
    )
    width = channels // group_count
    vmem = pl.BlockSpec(memory_space=pltpu.VMEM)
    return pl.pallas_call(
        lambda *refs: conv_kernel(*refs, group_width=width),
        out_shape=(
            jax.ShapeDtypeStruct((rows, channels), jnp.bfloat16),
            jax.ShapeDtypeStruct((channels // DH, 3, rows, DH), jnp.bfloat16),
        ),
        in_specs=[vmem] * 7,
        out_specs=(vmem, vmem),
        cost_estimate=pl.CostEstimate(
            flops=2 * 2 * 2 * 8 * rows * rows * channels,
            transcendentals=0,
            bytes_accessed=16 * cur.size,
        ),
    )(prev, cur, padded, outer, bypass.reshape(1, channels), query_rows, key_rows)


def piece_scores(q, k_ref, i, xd, x, rows, row_id, col_id, inv_root):
    length = (i + 1) * rows
    dh = k_ref.shape[-1]
    k = k_ref[: i + 1].reshape(length, dh)
    s = lax.dot_general(
        q, k, (((1,), (1,)), ((), ())), preferred_element_type=jnp.float32
    ) * inv_root
    visible = (xd * rows + col_id) <= (x * rows + row_id)
    tail = jnp.where(visible, s[:, length - rows :], -1e30)
    head = s[:, : length - rows] if i > 0 else None
    return head, tail, visible


def piece_max(head, tail):
    m = jnp.max(tail, axis=1, keepdims=True)
    if head is not None:
        m = jnp.maximum(m, jnp.max(head, axis=1, keepdims=True))
    return m


def piece_sums(head, tail, visible, v_ref, i, highest, rows):
    dh = v_ref.shape[-1]
    w_tail = jnp.where(visible, jnp.exp(tail - highest), 0.0)
    part_sum = jnp.sum(w_tail, axis=1, keepdims=True)
    part = jnp.dot(w_tail.astype(jnp.bfloat16), v_ref[i], preferred_element_type=jnp.float32)
    if head is not None:
        w_head = jnp.exp(head - highest)
        part_sum = part_sum + jnp.sum(w_head, axis=1, keepdims=True)
        v_head = v_ref[:i].reshape(i * rows, dh)
        part = part + jnp.dot(
            w_head.astype(jnp.bfloat16), v_head, preferred_element_type=jnp.float32
        )
    return part_sum, part


def attend_first_kernel(x_ref, q_ref, *refs, offsets, nx):
    n = len(offsets)
    k_refs = refs[:n]
    v_refs = refs[n : 2 * n]
    m_ref, l_ref, acc_ref = refs[2 * n :]
    x = x_ref[0]
    blocks, rows, dh = q_ref.shape
    inv_root = 1.0 / math.sqrt(DH)
    row_id = lax.broadcasted_iota(jnp.int32, (rows, rows), 0)
    col_id = lax.broadcasted_iota(jnp.int32, (rows, rows), 1)
    for i in range(blocks):
        q = q_ref[i]
        pieces = []
        for j, d in enumerate(offsets):
            xd = lax.rem(x + d, nx)
            pieces.append(piece_scores(q, k_refs[j], i, xd, x, rows, row_id, col_id, inv_root))
        highest = None
        for head, tail, _ in pieces:
            m = piece_max(head, tail)
            highest = m if highest is None else jnp.maximum(highest, m)
        total = None
        acc = None
        for j, (head, tail, visible) in enumerate(pieces):
            part_sum, part = piece_sums(head, tail, visible, v_refs[j], i, highest, rows)
            total = part_sum if total is None else total + part_sum
            acc = part if acc is None else acc + part
        m_ref[i] = highest
        l_ref[i] = total
        acc_ref[i] = acc


def attend_last_kernel(x_ref, q_ref, k_ref, v_ref, m_ref, l_ref, acc_ref, o_ref, *, offset, nx):
    x = x_ref[0]
    blocks, rows, dh = q_ref.shape
    inv_root = 1.0 / math.sqrt(DH)
    row_id = lax.broadcasted_iota(jnp.int32, (rows, rows), 0)
    col_id = lax.broadcasted_iota(jnp.int32, (rows, rows), 1)
    xd = lax.rem(x + offset, nx)
    for i in range(blocks):
        head, tail, visible = piece_scores(q_ref[i], k_ref, i, xd, x, rows, row_id, col_id, inv_root)
        earlier = m_ref[i]
        highest = jnp.maximum(earlier, piece_max(head, tail))
        scale = jnp.exp(earlier - highest)
        part_sum, part = piece_sums(head, tail, visible, v_ref, i, highest, rows)
        total = l_ref[i] * scale + part_sum
        acc = acc_ref[i] * scale + part
        o_ref[i] = (acc / total).astype(o_ref.dtype)


def attend_local(x_index, q, ks, vs, nx):
    blocks, rows, dh = q.shape
    seq = nx * blocks * rows
    vmem = pl.BlockSpec(memory_space=pltpu.VMEM)
    smem = pl.BlockSpec(memory_space=pltpu.SMEM)
    params = pltpu.CompilerParams(vmem_limit_bytes=48 * 1024 * 1024)
    last = 2 if nx == 4 else nx - 1
    first = [d for d in range(nx) if d != last]
    share = blocks * rows * seq * dh // nx
    m, l, acc = pl.pallas_call(
        lambda *refs: attend_first_kernel(*refs, offsets=first, nx=nx),
        out_shape=(
            jax.ShapeDtypeStruct((blocks, rows, 1), jnp.float32),
            jax.ShapeDtypeStruct((blocks, rows, 1), jnp.float32),
            jax.ShapeDtypeStruct((blocks, rows, dh), jnp.float32),
        ),
        in_specs=[smem] + [vmem] * (1 + 2 * len(first)),
        out_specs=(vmem, vmem, vmem),
        compiler_params=params,
        cost_estimate=pl.CostEstimate(
            flops=2 * share * len(first),
            transcendentals=blocks * rows * seq * len(first) // (2 * nx),
            bytes_accessed=2 * q.size + 4 * seq * dh + 4 * q.size,
        ),
    )(x_index, q, *[ks[d] for d in first], *[vs[d] for d in first])
    return pl.pallas_call(
        lambda *refs: attend_last_kernel(*refs, offset=last, nx=nx),
        out_shape=jax.ShapeDtypeStruct(q.shape, jnp.bfloat16),
        in_specs=[smem] + [vmem] * 6,
        out_specs=vmem,
        compiler_params=params,
        cost_estimate=pl.CostEstimate(
            flops=2 * share,
            transcendentals=blocks * rows * seq // (2 * nx),
            bytes_accessed=2 * q.size + seq * dh + 8 * q.size,
        ),
    )(x_index, q, ks[last], vs[last], m, l, acc)


def gather_x(piece, nx, split_axis=0):
    if nx == 4:
        half = piece.shape[split_axis] // 2
        from_left = shifted(piece, "cx", 1)
        from_right = shifted(piece, "cx", -1)
        relay_a = shifted(lax.slice_in_dim(from_right, 0, half, axis=split_axis), "cx", -1)
        relay_b = shifted(
            lax.slice_in_dim(from_left, half, piece.shape[split_axis], axis=split_axis), "cx", 1
        )
        relay = jnp.concatenate([relay_a, relay_b], axis=split_axis)
        return [piece, from_right, relay, from_left]
    return [piece] + [shifted(piece, "cx", -d) for d in range(1, nx)]


def shards(inner_gate, outer_gate, signal, filters, bypass, query_rows, key_rows):
    local_rows, channels = signal.shape
    nz = lax.axis_size("cz")
    nx = lax.axis_size("cx")
    members = nz * nx
    heads = channels // DH
    my_x = lax.axis_index("cx")

    product = (inner_gate.astype(jnp.float32) * signal.astype(jnp.float32)).astype(jnp.bfloat16)
    previous = lax.ppermute(
        product,
        ("cz", "cx"),
        [(i, i + 1) for i in range(members - 1)],
    )
    hyena_out, qkv = hyena_local(previous, product, filters, outer_gate, bypass, query_rows, key_rows)

    spread = lax.all_to_all(qkv, "cz", 0, 0, tiled=True)
    q_here = spread[:, 0]
    got = gather_x(spread[:, 1:].transpose(1, 0, 2, 3), nx, 1)
    ks = [g[0] for g in got]
    vs = [g[1] for g in got]
    x_index = jnp.reshape(my_x, (1,)).astype(jnp.int32)
    out_here = attend_local(x_index, q_here, ks, vs, nx)
    returned = lax.all_to_all(out_here, "cz", 0, 0, tiled=True)
    attended = returned.transpose(1, 0, 2).reshape(local_rows, channels)
    return (hyena_out, attended)


def ctx_split(mesh):
    devices = np.asarray(mesh.devices)
    row = devices[0]
    try:
        nx = len({d.coords[0] for d in row})
    except Exception:
        nx = 4
    if row.size % nx:
        nx = 1
    return Mesh(devices.reshape(devices.shape[0], row.size // nx, nx), ("dp", "cz", "cx"))


def solution(mesh):
    split = ctx_split(mesh)
    rows = P(("dp", "cz", "cx"), None)
    placed = (rows, rows, rows, P(), P(), rows, rows)
    return jax.shard_map(
        shards,
        mesh=split,
        in_specs=placed,
        out_specs=(rows, rows),
        check_vma=False,
    )
```
